32 devices in a mesh: outer: 4 (over z), inner: 8 (over y, x, core).
Axes of the slice: x: 2, y: 2, z: 4, core: 2. Of those that a mesh axis runs over, the one named last changes fastest.
Arguments:
- observations: float32 [2048, 128], P(('outer', 'inner')), may hold values from -18 to 18
- gains: float32 [2048, 128, 128], P(('outer', 'inner')), may hold values from -0.2 to 0.7, as said below
- smoother_gains: float32 [2048, 128, 128], P(('outer', 'inner')), may hold values from -0.2 to 1.05, as said below
- transition: float32 [128, 128], replicated, may hold values from -0.2 to 1.05, as said below
- observation_map: float32 [128, 128], replicated, may hold values from -0.25 to 1.25, as said below
- initial_mean: float32 [128], replicated, may hold values from -12 to 12
Outputs:
- filtered: float32 [2048, 128], P(('outer', 'inner'))
- smoothed: float32 [2048, 128], P(('outer', 'inner'))
The draws below stay inside these ranges and needn't reach their ends.
Inputs may be any that keep to these rules, and one draw needn't show every extreme that they name: `gains`: each frame's gain is a dense 128 by 128 matrix with entries in this range; nothing else about its structure is promised. `smoother_gains`: each frame's smoother gain is a dense 128 by 128 matrix with entries in this range; nothing else about its structure is promised. `transition`: a dense 128 by 128 matrix. `observation_map`: a dense 128 by 128 matrix.
All inputs are finite; a program needn't handle non-finite values.
Results may differ from the reference program's by a relative error of at most 0.0003.
Values sent between devices are 32-bit elements; how exact they have to be, the bound alone decides.
No kernel may reach another device: no remote copies, remote signals or barrier semaphores. Data moves between devices by JAX's collectives and lax.ppermute only.
A program may use at most 128 MiB of HBM per device.

```python
import math
import jax
import jax.numpy as jnp
from jax import lax

STATE_ENTRIES = 128
FR = 64
FRAME_COUNT = 2048


def channel_layout(key):
    slow_share = 0.5
    gradual_mask = jax.random.uniform(jax.random.fold_in(key, 101), (STATE_ENTRIES,)) < slow_share
    quick_fraction = jnp.exp(jax.random.uniform(jax.random.fold_in(key, 102), (STATE_ENTRIES,), minval=math.log(1.0 / 50.0), maxval=math.log(1.0 / 30.0)))
    spike_frames = jax.random.randint(jax.random.fold_in(key, 103), (3,), 0, FRAME_COUNT)
    spike_rows = jnp.any(jnp.arange(FRAME_COUNT)[:, None] == spike_frames[None, :], axis=1)
    return (gradual_mask, quick_fraction, spike_rows)


def frame_factors(key, salt):
    roughness = jax.random.uniform(jax.random.fold_in(key, salt), (FRAME_COUNT, STATE_ENTRIES), minval=0.5, maxval=1.5)
    segment = 2.0 ** jax.random.uniform(jax.random.fold_in(key, salt + 1), (FRAME_COUNT // FR,), minval=-0.5, maxval=0.5)
    return roughness * jnp.repeat(segment, FR)[:, None]


def draw_gains(key, part):
    gradual_mask, quick_fraction, spike_rows = channel_layout(key)
    factors = frame_factors(key, 201)
    gain_fraction = jnp.where(gradual_mask[None, :], math.log(2.0) / (2.0 * FRAME_COUNT) * factors, quick_fraction[None, :] * factors)
    spike_level = jax.random.uniform(jax.random.fold_in(key, 203), (FRAME_COUNT, STATE_ENTRIES), minval=0.3, maxval=0.5)
    gain_fraction = jnp.where(spike_rows[:, None] & gradual_mask[None, :], spike_level, gain_fraction)
    jitter = jax.random.truncated_normal(jax.random.fold_in(key, 204), -4.0, 4.0, (FRAME_COUNT, STATE_ENTRIES, STATE_ENTRIES))
    result = gain_fraction[:, :, None] * (jnp.eye(STATE_ENTRIES, dtype=jnp.float32)[None] + 0.3 * jitter / math.sqrt(STATE_ENTRIES))
    return result.astype(jnp.float32)


def draw_smoother_gains(key, part):
    gradual_mask, quick_fraction, spike_rows = channel_layout(key)
    factors = frame_factors(key, 301)
    retained_flags = jnp.where(gradual_mask[None, :], jnp.exp(-(math.log(2.0) / (2.0 * FRAME_COUNT)) * factors), jnp.exp(-quick_fraction[None, :] * factors))
    spike_level = jax.random.uniform(jax.random.fold_in(key, 303), (FRAME_COUNT, STATE_ENTRIES), minval=0.5, maxval=0.8)
    retained_flags = jnp.where(spike_rows[:, None] & gradual_mask[None, :], spike_level, retained_flags)
    jitter = jax.random.truncated_normal(jax.random.fold_in(key, 304), -4.0, 4.0, (FRAME_COUNT, STATE_ENTRIES, STATE_ENTRIES))
    result = retained_flags[:, :, None] * jnp.eye(STATE_ENTRIES, dtype=jnp.float32)[None] + 0.3 * (1.0 - retained_flags)[:, :, None] * jitter / math.sqrt(STATE_ENTRIES)
    return result.astype(jnp.float32)


def draw_transition(key, part):
    gradual_mask, quick_fraction, spike_rows = channel_layout(key)
    slow_keep = jnp.exp(-jax.random.uniform(jax.random.fold_in(key, 401), (STATE_ENTRIES,), minval=0.2, maxval=1.0) * math.log(2.0) / (2.0 * FRAME_COUNT))
    fast_keep = jax.random.uniform(jax.random.fold_in(key, 402), (STATE_ENTRIES,), minval=0.9, maxval=0.99)
    retained_flags = jnp.where(gradual_mask, slow_keep, fast_keep)
    jitter = jax.random.truncated_normal(jax.random.fold_in(key, 403), -4.0, 4.0, (STATE_ENTRIES, STATE_ENTRIES))
    result = jnp.diag(retained_flags) + 0.3 * (1.0 - retained_flags)[:, None] * jitter / math.sqrt(STATE_ENTRIES)
    return result.astype(jnp.float32)


def draw_observation_map(key, part):
    jitter = jax.random.truncated_normal(jax.random.fold_in(key, 501), -4.0, 4.0, (STATE_ENTRIES, STATE_ENTRIES))
    result = jnp.eye(STATE_ENTRIES, dtype=jnp.float32) + 0.3 * jitter / math.sqrt(STATE_ENTRIES)
    return result.astype(jnp.float32)


def levels(stream_key, shape, shards, smallest, largest):
    def one(axis_at, shards_of):
        draws = jax.random.uniform(jax.random.fold_in(jax.random.fold_in(stream_key, 6), axis_at), (shards_of,), jnp.float32, smallest / len(shards), largest / len(shards))
        return jnp.repeat(jnp.exp(draws), shape[axis_at] // shards_of).reshape((-1,) + (1,) * (len(shape) - axis_at - 1))

    factor_of = one(*shards[0])
    for cut in shards[1:]:
        factor_of = factor_of * one(*cut)
    return factor_of


def noise(stream_key, dims, scale, most, split=(), held_as=jnp.bfloat16):
    array = jax.random.normal(stream_key, dims, jnp.float32) * scale
    if len(split) > 0:
        array = levels(stream_key, dims, split, -0.22, 0.18) * array
    return jnp.clip(array, min=-most, max=most).astype(held_as)


def setup_inputs(seed: int = 0) -> dict:
    key_of = jax.random.split(jax.random.key(seed), 7)
    return {
        "observations": noise(key_of[0], (FRAME_COUNT, STATE_ENTRIES), 3.0, 18.0, ((0, 32),), jnp.float32),
        "gains": draw_gains(jax.random.fold_in(key_of[6], 71), 0),
        "smoother_gains": draw_smoother_gains(jax.random.fold_in(key_of[6], 71), 0),
        "transition": draw_transition(jax.random.fold_in(key_of[6], 71), 0),
        "observation_map": draw_observation_map(jax.random.fold_in(key_of[6], 71), 0),
        "initial_mean": noise(key_of[5], (STATE_ENTRIES,), 2.0, 12.0, (), jnp.float32),
    }


exact = lax.Precision.HIGHEST


def reference(observations, gains, smoother_gains, transition, observation_map, initial_mean):
    def forward_step(mean_state, element):
        observed, gain_now = element
        predicted = jnp.dot(transition, mean_state, precision=exact, preferred_element_type=jnp.float32)
        innovation = observed - jnp.dot(observation_map, predicted, precision=exact, preferred_element_type=jnp.float32)
        updated = predicted + jnp.dot(gain_now, innovation, precision=exact, preferred_element_type=jnp.float32)
        return updated, updated

    _, filtered = lax.scan(forward_step, initial_mean, (observations, gains))
    predicted_all = jnp.dot(filtered, transition.T, precision=exact, preferred_element_type=jnp.float32)
    offsets = filtered - jnp.einsum("tij,tj->ti", smoother_gains, predicted_all, precision=exact, preferred_element_type=jnp.float32)

    def backward_step(later_state, element):
        gain_now, offset_now = element
        current = jnp.dot(gain_now, later_state, precision=exact, preferred_element_type=jnp.float32) + offset_now
        return current, current

    final_state = filtered[-1]
    _, heading = lax.scan(backward_step, final_state, (smoother_gains[:-1], offsets[:-1]), reverse=True)
    smoothed = jnp.concatenate((heading, final_state[None, :]), axis=0)
    return filtered, smoothed
```

```python
import jax
import jax.numpy as jnp
from jax import lax
from jax.sharding import PartitionSpec as P

exact = lax.Precision.HIGHEST
AXES = ("outer", "inner")


def mm(a, b):
    return jnp.matmul(a, b, precision=exact, preferred_element_type=jnp.float32)


def mv(a, v):
    return jnp.einsum("...ij,...j->...i", a, v, precision=exact, preferred_element_type=jnp.float32)


def matrix_tree(matrices):
    tiers = [matrices]
    depth = matrices.shape[0].bit_length() - 1
    for height in range(depth):
        below = tiers[-1]
        paired = below.reshape(below.shape[0] // 2, 2, below.shape[1], below.shape[2])
        tiers.append(mm(paired[:, 1], paired[:, 0]))
    return tiers


def vector_tree(tiers, vectors):
    sums = [vectors]
    for height in range(len(tiers) - 1):
        below = sums[-1]
        paired = below.reshape(below.shape[0] // 2, 2, below.shape[1])
        matrices = tiers[height]
        later_maps = matrices.reshape(
            matrices.shape[0] // 2, 2, matrices.shape[1], matrices.shape[2]
        )[:, 1]
        sums.append(mv(later_maps, paired[:, 0]) + paired[:, 1])
    return sums


def spread(tiers, sums, entry_state):
    states = entry_state[None, :]
    state_width = entry_state.shape[0]
    for height in reversed(range(len(tiers) - 1)):
        matrices = tiers[height]
        left_maps = matrices.reshape(matrices.shape[0] // 2, 2, state_width, state_width)[:, 0]
        left_offsets = sums[height].reshape(matrices.shape[0] // 2, 2, state_width)[:, 0]
        right_states = mv(left_maps, states) + left_offsets
        states = jnp.stack((states, right_states), axis=1).reshape(-1, state_width)
    return mv(tiers[0], states) + sums[0]


def pad_pow2(mats, vecs, count):
    size = 1
    while size < count:
        size *= 2
    width = mats.shape[-1]
    if size > count:
        eye = jnp.broadcast_to(jnp.eye(width, dtype=mats.dtype), (size - count, width, width))
        mats = jnp.concatenate((mats, eye), axis=0)
        vecs = jnp.concatenate((vecs, jnp.zeros((size - count, width), vecs.dtype)), axis=0)
    return mats, vecs


def entry_from_left(mats, vecs, start, me):
    count = mats.shape[0]
    width = mats.shape[-1]
    ahead = (jnp.arange(count) < me)
    eye = jnp.eye(width, dtype=jnp.float32)
    mats = jnp.where(ahead[:, None, None], mats, eye[None])
    vecs = jnp.where(ahead[:, None], vecs, 0.0)
    first = mv(mats[0], start) + vecs[0]
    vecs = vecs.at[0].set(first)
    mats = mats.at[0].set(jnp.zeros_like(eye))
    mats, vecs = pad_pow2(mats, vecs, count)
    while mats.shape[0] > 1:
        pm = mats.reshape(mats.shape[0] // 2, 2, width, width)
        pv = vecs.reshape(vecs.shape[0] // 2, 2, width)
        vecs = mv(pm[:, 1], pv[:, 0]) + pv[:, 1]
        mats = mm(pm[:, 1], pm[:, 0])
    return vecs[0]


def prefix_weights(mats, me):
    count = mats.shape[0]
    width = mats.shape[-1]
    index = jnp.arange(count)
    eye = jnp.eye(width, dtype=jnp.float32)
    masked = jnp.where((index > me)[:, None, None], mats, eye[None])
    inclusive = masked
    step = 1
    while step < count:
        shifted = jnp.concatenate(
            (jnp.broadcast_to(eye, (step, width, width)), inclusive[: count - step]), axis=0
        )
        inclusive = mm(shifted, inclusive)
        step *= 2
    exclusive = jnp.concatenate((eye[None], inclusive[: count - 1]), axis=0)
    return jnp.where((index > me)[:, None, None], exclusive, 0.0)


def on_device(observations, gains, smoother_gains, transition, observation_map, initial_mean):
    frames = observations.shape[0]
    me = lax.axis_index(AXES)
    devices = lax.axis_size(AXES)
    mapped = mm(observation_map, transition)
    forward_maps = transition[None] - jnp.einsum(
        "tij,jk->tik", gains, mapped, precision=exact, preferred_element_type=jnp.float32
    )
    forward_inputs = mv(gains, observations)
    forward_tiers = matrix_tree(forward_maps)
    forward_sums = vector_tree(forward_tiers, forward_inputs)
    packed = jnp.concatenate((forward_tiers[-1][0], forward_sums[-1][0][None, :]), axis=0)
    gathered = lax.all_gather(packed, AXES)

    global_frame = me * frames + jnp.arange(frames, dtype=jnp.int32)
    final_frame = global_frame == frames * devices - 1
    masked_gains = jnp.where(
        final_frame[:, None, None], jnp.zeros_like(smoother_gains), smoother_gains
    )
    backward_tiers = matrix_tree(masked_gains[::-1])
    gathered_back = lax.all_gather(backward_tiers[-1][0], AXES)
    weights = prefix_weights(gathered_back, me)

    entry_state = entry_from_left(gathered[:, :-1], gathered[:, -1], initial_mean, me)
    filtered = spread(forward_tiers, forward_sums, entry_state)
    predicted_all = jnp.dot(
        filtered, transition.T, precision=exact, preferred_element_type=jnp.float32
    )
    offsets = filtered - mv(masked_gains, predicted_all)
    backward_sums = vector_tree(backward_tiers, offsets[::-1])
    gathered_offsets = lax.all_gather(backward_sums[-1][0], AXES)
    after_state = jnp.sum(mv(weights, gathered_offsets), axis=0)
    smoothed = spread(backward_tiers, backward_sums, after_state)[::-1]
    return (filtered, smoothed)


def solution(mesh):
    in_specs = (
        P(AXES, None),
        P(AXES, None, None),
        P(AXES, None, None),
        P(),
        P(),
        P(),
    )
    out_specs = (P(AXES, None), P(AXES, None))
    return jax.shard_map(
        on_device, mesh=mesh, in_specs=in_specs, out_specs=out_specs, check_vma=False
    )
```

```python
import jax
import jax.numpy as jnp
from jax import lax
from jax.sharding import PartitionSpec as P

exact = lax.Precision.HIGHEST
AXES = ("outer", "inner")


def mm(a, b):
    return jnp.matmul(a, b, precision=exact, preferred_element_type=jnp.float32)


def mv(a, v):
    return jnp.einsum("...ij,...j->...i", a, v, precision=exact, preferred_element_type=jnp.float32)


def pair_up(mats, vecs, backward):
    shape = mats.shape
    pm = mats.reshape(shape[:-3] + (shape[-3] // 2, 2) + shape[-2:])
    pv = vecs.reshape(vecs.shape[:-2] + (vecs.shape[-2] // 2, 2, vecs.shape[-1]))
    first, second = (1, 0) if backward else (0, 1)
    m1, m2 = pm[..., first, :, :], pm[..., second, :, :]
    v1, v2 = pv[..., first, :], pv[..., second, :]
    return mm(m2, m1), mv(m2, v1) + v2


def local_tiers(mats, vecs, backward):
    tiers = [(mats, vecs)]
    while tiers[-1][0].shape[0] > 1:
        tiers.append(pair_up(tiers[-1][0], tiers[-1][1], backward))
    return tiers


def spread(tiers, entry, backward):
    width = entry.shape[0]
    states = entry[None, :]
    for height in reversed(range(len(tiers) - 1)):
        mats, vecs = tiers[height]
        half = mats.shape[0] // 2
        pm = mats.reshape(half, 2, width, width)
        pv = vecs.reshape(half, 2, width)
        if backward:
            other = mv(pm[:, 1], states) + pv[:, 1]
            states = jnp.stack((other, states), axis=1)
        else:
            other = mv(pm[:, 0], states) + pv[:, 0]
            states = jnp.stack((states, other), axis=1)
        states = states.reshape(-1, width)
    return mv(tiers[0][0], states) + tiers[0][1]


def pad_pow2(mats, vecs):
    count = mats.shape[-3]
    size = 1
    while size < count:
        size *= 2
    if size > count:
        width = mats.shape[-1]
        eye = jnp.broadcast_to(
            jnp.eye(width, dtype=mats.dtype), mats.shape[:-3] + (size - count, width, width)
        )
        mats = jnp.concatenate((mats, eye), axis=-3)
        zero = jnp.zeros(vecs.shape[:-2] + (size - count, width), vecs.dtype)
        vecs = jnp.concatenate((vecs, zero), axis=-2)
    return mats, vecs


def reduce_maps(mats, vecs, backward):
    mats, vecs = pad_pow2(mats, vecs)
    while mats.shape[-3] > 1:
        mats, vecs = pair_up(mats, vecs, backward)
    return mats[..., 0, :, :], vecs[..., 0, :]


def keep_only(mats, vecs, keep):
    eye = jnp.eye(mats.shape[-1], dtype=jnp.float32)
    mats = jnp.where(keep[:, None, None], mats, eye)
    vecs = jnp.where(keep[:, None], vecs, 0.0)
    return mats, vecs


def pack(mat, vec):
    return jnp.concatenate((mat, vec[None, :]), axis=0)


def group_level(mat, vec, axis, backward):
    gathered = lax.all_gather(pack(mat, vec), axis)
    mats, vecs = gathered[:, :-1], gathered[:, -1]
    me = lax.axis_index(axis)
    index = jnp.arange(mats.shape[0])
    keep = index > me if backward else index < me
    pm, pv = keep_only(mats, vecs, keep)
    both_m = jnp.stack((pm, mats), axis=0)
    both_v = jnp.stack((pv, vecs), axis=0)
    rm, rv = reduce_maps(both_m, both_v, backward)
    return (rm[0], rv[0]), (rm[1], rv[1])


def across(mat, vec, backward):
    (pm, pv), (gm, gv) = group_level(mat, vec, "inner", backward)
    gathered = lax.all_gather(pack(gm, gv), "outer")
    mats, vecs = gathered[:, :-1], gathered[:, -1]
    me = lax.axis_index("outer")
    index = jnp.arange(mats.shape[0])
    keep = index > me if backward else index < me
    om, ov = reduce_maps(*keep_only(mats, vecs, keep), backward)
    return mm(pm, om), mv(pm, ov) + pv


def on_device(observations, gains, smoother_gains, transition, observation_map, initial_mean):
    me = lax.axis_index(AXES)
    devices = lax.axis_size(AXES)
    mapped = mm(observation_map, transition)
    forward_maps = transition[None] - jnp.einsum(
        "tij,jk->tik", gains, mapped, precision=exact, preferred_element_type=jnp.float32
    )
    forward_inputs = mv(gains, observations)
    forward = local_tiers(forward_maps, forward_inputs, False)
    fm, fv = forward[-1][0][0], forward[-1][1][0]
    before_m, before_v = across(fm, fv, False)
    entry_state = mv(before_m, initial_mean) + before_v
    filtered = spread(forward, entry_state, False)

    predicted_all = jnp.dot(
        filtered, transition.T, precision=exact, preferred_element_type=jnp.float32
    )
    offsets = filtered - mv(smoother_gains, predicted_all)
    backward = local_tiers(smoother_gains, offsets, True)
    bm, bv = backward[-1][0][0], backward[-1][1][0]
    last = me == devices - 1
    extra = jnp.where(last, predicted_all[-1], 0.0)
    bv = bv + mv(bm, extra)
    after_m, after_v = across(bm, bv, True)
    after_state = after_v + extra
    smoothed = spread(backward, after_state, True)
    return (filtered, smoothed)


def solution(mesh):
    in_specs = (
        P(AXES, None),
        P(AXES, None, None),
        P(AXES, None, None),
        P(),
        P(),
        P(),
    )
    out_specs = (P(AXES, None), P(AXES, None))
    return jax.shard_map(
        on_device, mesh=mesh, in_specs=in_specs, out_specs=out_specs, check_vma=False
    )
```

```python
import jax
import jax.numpy as jnp
from jax import lax
from jax.sharding import PartitionSpec as P

exact = lax.Precision.HIGHEST
AXES = ("outer", "inner")


def mm(a, b):
    return jnp.matmul(a, b, precision=exact, preferred_element_type=jnp.float32)


def mv(a, v):
    return jnp.sum(a * v[..., None, :], axis=-1)


def pair_up(mats, vecs, backward):
    shape = mats.shape
    pm = mats.reshape(shape[:-3] + (shape[-3] // 2, 2) + shape[-2:])
    pv = vecs.reshape(vecs.shape[:-2] + (vecs.shape[-2] // 2, 2, vecs.shape[-1]))
    first, second = (1, 0) if backward else (0, 1)
    m1, m2 = pm[..., first, :, :], pm[..., second, :, :]
    v1, v2 = pv[..., first, :], pv[..., second, :]
    return mm(m2, m1), mv(m2, v1) + v2


def local_tiers(mats, vecs, backward):
    tiers = [(mats, vecs)]
    while tiers[-1][0].shape[0] > 1:
        tiers.append(pair_up(tiers[-1][0], tiers[-1][1], backward))
    return tiers


def spread(tiers, entry, backward):
    width = entry.shape[0]
    states = entry[None, :]
    for height in reversed(range(len(tiers) - 1)):
        mats, vecs = tiers[height]
        half = mats.shape[0] // 2
        pm = mats.reshape(half, 2, width, width)
        pv = vecs.reshape(half, 2, width)
        if backward:
            other = mv(pm[:, 1], states) + pv[:, 1]
            states = jnp.stack((other, states), axis=1)
        else:
            other = mv(pm[:, 0], states) + pv[:, 0]
            states = jnp.stack((states, other), axis=1)
        states = states.reshape(-1, width)
    return mv(tiers[0][0], states) + tiers[0][1]


def pad_pow2(mats, vecs):
    count = mats.shape[-3]
    size = 1
    while size < count:
        size *= 2
    if size > count:
        width = mats.shape[-1]
        eye = jnp.broadcast_to(
            jnp.eye(width, dtype=mats.dtype), mats.shape[:-3] + (size - count, width, width)
        )
        mats = jnp.concatenate((mats, eye), axis=-3)
        zero = jnp.zeros(vecs.shape[:-2] + (size - count, width), vecs.dtype)
        vecs = jnp.concatenate((vecs, zero), axis=-2)
    return mats, vecs


def reduce_maps(mats, vecs, backward):
    mats, vecs = pad_pow2(mats, vecs)
    while mats.shape[-3] > 1:
        mats, vecs = pair_up(mats, vecs, backward)
    return mats[..., 0, :, :], vecs[..., 0, :]


def keep_only(mats, vecs, keep):
    eye = jnp.eye(mats.shape[-1], dtype=jnp.float32)
    mats = jnp.where(keep[:, None, None], mats, eye)
    vecs = jnp.where(keep[:, None], vecs, 0.0)
    return mats, vecs


def pack(mat, vec):
    return jnp.concatenate((mat, vec[None, :]), axis=0)


def group_level(mat, vec, axis, backward):
    gathered = lax.all_gather(pack(mat, vec), axis)
    mats, vecs = gathered[:, :-1], gathered[:, -1]
    me = lax.axis_index(axis)
    index = jnp.arange(mats.shape[0])
    keep = index > me if backward else index < me
    pm, pv = keep_only(mats, vecs, keep)
    both_m = jnp.stack((pm, mats), axis=0)
    both_v = jnp.stack((pv, vecs), axis=0)
    rm, rv = reduce_maps(both_m, both_v, backward)
    return (rm[0], rv[0]), (rm[1], rv[1])


def across(mat, vec, backward):
    (pm, pv), (gm, gv) = group_level(mat, vec, "inner", backward)
    gathered = lax.all_gather(pack(gm, gv), "outer")
    mats, vecs = gathered[:, :-1], gathered[:, -1]
    me = lax.axis_index("outer")
    index = jnp.arange(mats.shape[0])
    keep = index > me if backward else index < me
    om, ov = reduce_maps(*keep_only(mats, vecs, keep), backward)
    return mm(pm, om), mv(pm, ov) + pv


def on_device(observations, gains, smoother_gains, transition, observation_map, initial_mean):
    me = lax.axis_index(AXES)
    devices = lax.axis_size(AXES)
    mapped = mm(observation_map, transition)
    forward_maps = transition[None] - jnp.einsum(
        "tij,jk->tik", gains, mapped, precision=exact, preferred_element_type=jnp.float32
    )
    forward_inputs = mv(gains, observations)
    forward = local_tiers(forward_maps, forward_inputs, False)
    fm, fv = forward[-1][0][0], forward[-1][1][0]
    before_m, before_v = across(fm, fv, False)
    entry_state = mv(before_m, initial_mean) + before_v
    filtered = spread(forward, entry_state, False)

    predicted_all = jnp.dot(
        filtered, transition.T, precision=exact, preferred_element_type=jnp.float32
    )
    offsets = filtered - mv(smoother_gains, predicted_all)
    backward = local_tiers(smoother_gains, offsets, True)
    bm, bv = backward[-1][0][0], backward[-1][1][0]
    last = me == devices - 1
    extra = jnp.where(last, predicted_all[-1], 0.0)
    bv = bv + mv(bm, extra)
    after_m, after_v = across(bm, bv, True)
    after_state = after_v + extra
    smoothed = spread(backward, after_state, True)
    return (filtered, smoothed)


def solution(mesh):
    in_specs = (
        P(AXES, None),
        P(AXES, None, None),
        P(AXES, None, None),
        P(),
        P(),
        P(),
    )
    out_specs = (P(AXES, None), P(AXES, None))
    return jax.shard_map(
        on_device, mesh=mesh, in_specs=in_specs, out_specs=out_specs, check_vma=False
    )
```

```python
import jax
import jax.numpy as jnp
from jax import lax
from jax.sharding import PartitionSpec as P

exact = lax.Precision.HIGHEST
AXES = ("outer", "inner")


def mm(a, b):
    return jnp.matmul(a, b, precision=exact, preferred_element_type=jnp.float32)


def mv(a, v):
    return jnp.einsum("...ij,...j->...i", a, v, precision=exact, preferred_element_type=jnp.float32)


def mv_whole(a, v):
    return jnp.sum(a * v[..., None, :], axis=-1)


def pair_up(mats, vecs, backward):
    shape = mats.shape
    pm = mats.reshape(shape[:-3] + (shape[-3] // 2, 2) + shape[-2:])
    pv = vecs.reshape(vecs.shape[:-2] + (vecs.shape[-2] // 2, 2, vecs.shape[-1]))
    first, second = (1, 0) if backward else (0, 1)
    m1, m2 = pm[..., first, :, :], pm[..., second, :, :]
    v1, v2 = pv[..., first, :], pv[..., second, :]
    return mm(m2, m1), mv(m2, v1) + v2


def local_tiers(mats, vecs, backward):
    tiers = [(mats, vecs)]
    while tiers[-1][0].shape[0] > 1:
        tiers.append(pair_up(tiers[-1][0], tiers[-1][1], backward))
    return tiers


def spread(tiers, entry, backward):
    width = entry.shape[0]
    states = entry[None, :]
    for height in reversed(range(len(tiers) - 1)):
        mats, vecs = tiers[height]
        half = mats.shape[0] // 2
        pm = mats.reshape(half, 2, width, width)
        pv = vecs.reshape(half, 2, width)
        if backward:
            other = mv(pm[:, 1], states) + pv[:, 1]
            states = jnp.stack((other, states), axis=1)
        else:
            other = mv(pm[:, 0], states) + pv[:, 0]
            states = jnp.stack((states, other), axis=1)
        states = states.reshape(-1, width)
    return mv_whole(tiers[0][0], states) + tiers[0][1]


def pad_pow2(mats, vecs):
    count = mats.shape[-3]
    size = 1
    while size < count:
        size *= 2
    if size > count:
        width = mats.shape[-1]
        eye = jnp.broadcast_to(
            jnp.eye(width, dtype=mats.dtype), mats.shape[:-3] + (size - count, width, width)
        )
        mats = jnp.concatenate((mats, eye), axis=-3)
        zero = jnp.zeros(vecs.shape[:-2] + (size - count, width), vecs.dtype)
        vecs = jnp.concatenate((vecs, zero), axis=-2)
    return mats, vecs


def reduce_maps(mats, vecs, backward):
    mats, vecs = pad_pow2(mats, vecs)
    while mats.shape[-3] > 1:
        mats, vecs = pair_up(mats, vecs, backward)
    return mats[..., 0, :, :], vecs[..., 0, :]


def keep_only(mats, vecs, keep):
    eye = jnp.eye(mats.shape[-1], dtype=jnp.float32)
    mats = jnp.where(keep[:, None, None], mats, eye)
    vecs = jnp.where(keep[:, None], vecs, 0.0)
    return mats, vecs


def pack(mat, vec):
    return jnp.concatenate((mat, vec[None, :]), axis=0)


def group_level(mat, vec, axis, backward):
    gathered = lax.all_gather(pack(mat, vec), axis)
    mats, vecs = gathered[:, :-1], gathered[:, -1]
    me = lax.axis_index(axis)
    index = jnp.arange(mats.shape[0])
    keep = index > me if backward else index < me
    pm, pv = keep_only(mats, vecs, keep)
    both_m = jnp.stack((pm, mats), axis=0)
    both_v = jnp.stack((pv, vecs), axis=0)
    rm, rv = reduce_maps(both_m, both_v, backward)
    return (rm[0], rv[0]), (rm[1], rv[1])


def across(mat, vec, backward):
    (pm, pv), (gm, gv) = group_level(mat, vec, "inner", backward)
    gathered = lax.all_gather(pack(gm, gv), "outer")
    mats, vecs = gathered[:, :-1], gathered[:, -1]
    me = lax.axis_index("outer")
    index = jnp.arange(mats.shape[0])
    keep = index > me if backward else index < me
    om, ov = reduce_maps(*keep_only(mats, vecs, keep), backward)
    return mm(pm, om), mv(pm, ov) + pv


def on_device(observations, gains, smoother_gains, transition, observation_map, initial_mean):
    me = lax.axis_index(AXES)
    devices = lax.axis_size(AXES)
    mapped = mm(observation_map, transition)
    forward_maps = transition[None] - jnp.einsum(
        "tij,jk->tik", gains, mapped, precision=exact, preferred_element_type=jnp.float32
    )
    forward_inputs = mv_whole(gains, observations)
    forward = local_tiers(forward_maps, forward_inputs, False)
    fm, fv = forward[-1][0][0], forward[-1][1][0]
    before_m, before_v = across(fm, fv, False)
    entry_state = mv(before_m, initial_mean) + before_v
    filtered = spread(forward, entry_state, False)

    predicted_all = jnp.dot(
        filtered, transition.T, precision=exact, preferred_element_type=jnp.float32
    )
    offsets = filtered - mv_whole(smoother_gains, predicted_all)
    backward = local_tiers(smoother_gains, offsets, True)
    bm, bv = backward[-1][0][0], backward[-1][1][0]
    last = me == devices - 1
    extra = jnp.where(last, predicted_all[-1], 0.0)
    bv = bv + mv(bm, extra)
    after_m, after_v = across(bm, bv, True)
    after_state = after_v + extra
    smoothed = spread(backward, after_state, True)
    return (filtered, smoothed)


def solution(mesh):
    in_specs = (
        P(AXES, None),
        P(AXES, None, None),
        P(AXES, None, None),
        P(),
        P(),
        P(),
    )
    out_specs = (P(AXES, None), P(AXES, None))
    return jax.shard_map(
        on_device, mesh=mesh, in_specs=in_specs, out_specs=out_specs, check_vma=False
    )
```

```python
import jax
import jax.numpy as jnp
from jax import lax
from jax.sharding import PartitionSpec as P

exact = lax.Precision.HIGHEST
AXES = ("outer", "inner")


def mm(a, b):
    return jnp.matmul(a, b, precision=exact, preferred_element_type=jnp.float32)


def mv(a, v):
    return jnp.einsum("...ij,...j->...i", a, v, precision=exact, preferred_element_type=jnp.float32)


def mv_whole(a, v):
    return jnp.sum(a * v[..., None, :], axis=-1)


def pair_up(mats, vecs, backward):
    shape = mats.shape
    pm = mats.reshape(shape[:-3] + (shape[-3] // 2, 2) + shape[-2:])
    pv = vecs.reshape(vecs.shape[:-2] + (vecs.shape[-2] // 2, 2, vecs.shape[-1]))
    first, second = (1, 0) if backward else (0, 1)
    m1, m2 = pm[..., first, :, :], pm[..., second, :, :]
    v1, v2 = pv[..., first, :], pv[..., second, :]
    return mm(m2, m1), mv(m2, v1) + v2


def local_tiers(mats, vecs, backward):
    tiers = [(mats, vecs)]
    while tiers[-1][0].shape[0] > 1:
        tiers.append(pair_up(tiers[-1][0], tiers[-1][1], backward))
    return tiers


def spread(tiers, entry, backward):
    width = entry.shape[0]
    states = entry[None, :]
    for height in reversed(range(len(tiers) - 1)):
        mats, vecs = tiers[height]
        half = mats.shape[0] // 2
        pm = mats.reshape(half, 2, width, width)
        pv = vecs.reshape(half, 2, width)
        if backward:
            other = mv(pm[:, 1], states) + pv[:, 1]
            states = jnp.stack((other, states), axis=1)
        else:
            other = mv(pm[:, 0], states) + pv[:, 0]
            states = jnp.stack((states, other), axis=1)
        states = states.reshape(-1, width)
    return mv_whole(tiers[0][0], states) + tiers[0][1]


def compose_aug(second, first):
    width = second.shape[-2]
    joined = jnp.einsum(
        "...ij,...jk->...ik", second[..., :width], first,
        precision=exact, preferred_element_type=jnp.float32,
    )
    return joined.at[..., width].add(second[..., width])


def reduce_aug(maps, backward):
    count = maps.shape[-3]
    size = 1
    while size < count:
        size *= 2
    width = maps.shape[-2]
    ident = identity_aug(width)
    if size > count:
        pad = jnp.broadcast_to(ident, maps.shape[:-3] + (size - count,) + ident.shape)
        maps = jnp.concatenate((maps, pad), axis=-3)
    while maps.shape[-3] > 1:
        shape = maps.shape
        paired = maps.reshape(shape[:-3] + (shape[-3] // 2, 2) + shape[-2:])
        first, second = (1, 0) if backward else (0, 1)
        maps = compose_aug(paired[..., second, :, :], paired[..., first, :, :])
    return maps[..., 0, :, :]


def identity_aug(width):
    return jnp.concatenate(
        (jnp.eye(width, dtype=jnp.float32), jnp.zeros((width, 1), jnp.float32)), axis=1
    )


def keep_only(maps, keep):
    return jnp.where(keep[:, None, None], maps, identity_aug(maps.shape[-2]))


def apply_aug(block, state):
    width = block.shape[-2]
    return jnp.sum(block[:, :width] * state[None, :], axis=-1) + block[:, width]


def before_me(maps, axis, backward):
    me = lax.axis_index(axis)
    index = jnp.arange(maps.shape[0])
    keep = index > me if backward else index < me
    return keep_only(maps, keep)


def across(mat, vec, start, backward):
    mine = jnp.concatenate((mat, vec[:, None]), axis=1)
    group = lax.all_gather(mine, "inner")
    both = jnp.stack((before_me(group, "inner", backward), group), axis=0)
    part, whole = reduce_aug(both, backward)
    groups = lax.all_gather(whole, "outer")
    outer = reduce_aug(before_me(groups, "outer", backward), backward)
    return apply_aug(part, apply_aug(outer, start))


def on_device(observations, gains, smoother_gains, transition, observation_map, initial_mean):
    me = lax.axis_index(AXES)
    devices = lax.axis_size(AXES)
    mapped = mm(observation_map, transition)
    forward_maps = transition[None] - jnp.einsum(
        "tij,jk->tik", gains, mapped, precision=exact, preferred_element_type=jnp.float32
    )
    forward_inputs = mv_whole(gains, observations)
    forward = local_tiers(forward_maps, forward_inputs, False)
    fm, fv = forward[-1][0][0], forward[-1][1][0]
    entry_state = across(fm, fv, initial_mean, False)
    filtered = spread(forward, entry_state, False)

    predicted_all = jnp.dot(
        filtered, transition.T, precision=exact, preferred_element_type=jnp.float32
    )
    offsets = filtered - mv_whole(smoother_gains, predicted_all)
    backward = local_tiers(smoother_gains, offsets, True)
    bm, bv = backward[-1][0][0], backward[-1][1][0]
    last = me == devices - 1
    extra = jnp.where(last, predicted_all[-1], 0.0)
    bv = bv + mv(bm, extra)
    after_state = across(bm, bv, jnp.zeros_like(extra), True) + extra
    smoothed = spread(backward, after_state, True)
    return (filtered, smoothed)


def solution(mesh):
    in_specs = (
        P(AXES, None),
        P(AXES, None, None),
        P(AXES, None, None),
        P(),
        P(),
        P(),
    )
    out_specs = (P(AXES, None), P(AXES, None))
    return jax.shard_map(
        on_device, mesh=mesh, in_specs=in_specs, out_specs=out_specs, check_vma=False
    )
```

```python
import jax
import jax.numpy as jnp
from jax import lax
from jax.sharding import PartitionSpec as P

exact = lax.Precision.HIGHEST
AXES = ("outer", "inner")


def mm(a, b):
    return jnp.matmul(a, b, precision=exact, preferred_element_type=jnp.float32)


def mv(a, v):
    return jnp.einsum("...ij,...j->...i", a, v, precision=exact, preferred_element_type=jnp.float32)


def mv_whole(a, v):
    return jnp.sum(a * v[..., None, :], axis=-1)


def local_pair(mats, vecs, backward):
    count, width = mats.shape[0], mats.shape[-1]
    pm = mats.reshape(count // 2, 2, width, width)
    pv = vecs.reshape(count // 2, 2, width)
    first, second = (1, 0) if backward else (0, 1)
    joined = mm(pm[:, second], pm[:, first])
    partner = jnp.stack((pv[:, 1], pv[:, 0]), axis=1).reshape(count, width)
    crossed = mv_whole(mats, partner).reshape(count // 2, 2, width)
    return joined, crossed[:, second] + pv[:, second]


def pair_up(mats, vecs, backward):
    shape = mats.shape
    pm = mats.reshape(shape[:-3] + (shape[-3] // 2, 2) + shape[-2:])
    pv = vecs.reshape(vecs.shape[:-2] + (vecs.shape[-2] // 2, 2, vecs.shape[-1]))
    first, second = (1, 0) if backward else (0, 1)
    m1, m2 = pm[..., first, :, :], pm[..., second, :, :]
    v1, v2 = pv[..., first, :], pv[..., second, :]
    return mm(m2, m1), mv(m2, v1) + v2


def local_tiers(mats, vecs, backward):
    tiers = [(mats, vecs)]
    while tiers[-1][0].shape[0] > 1:
        tiers.append(local_pair(tiers[-1][0], tiers[-1][1], backward))
    return tiers


def spread(tiers, entry, backward):
    width = entry.shape[0]
    states = entry[None, :]
    for height in reversed(range(len(tiers) - 1)):
        mats, vecs = tiers[height]
        half = mats.shape[0] // 2
        pv = vecs.reshape(half, 2, width)
        both = jnp.broadcast_to(states[:, None, :], (half, 2, width)).reshape(-1, width)
        applied = mv_whole(mats, both).reshape(half, 2, width)
        if backward:
            other = applied[:, 1] + pv[:, 1]
            states = jnp.stack((other, states), axis=1)
        else:
            other = applied[:, 0] + pv[:, 0]
            states = jnp.stack((states, other), axis=1)
        states = states.reshape(-1, width)
    return mv_whole(tiers[0][0], states) + tiers[0][1]


def pad_pow2(mats, vecs):
    count = mats.shape[-3]
    size = 1
    while size < count:
        size *= 2
    if size > count:
        width = mats.shape[-1]
        eye = jnp.broadcast_to(
            jnp.eye(width, dtype=mats.dtype), mats.shape[:-3] + (size - count, width, width)
        )
        mats = jnp.concatenate((mats, eye), axis=-3)
        zero = jnp.zeros(vecs.shape[:-2] + (size - count, width), vecs.dtype)
        vecs = jnp.concatenate((vecs, zero), axis=-2)
    return mats, vecs


def reduce_maps(mats, vecs, backward):
    mats, vecs = pad_pow2(mats, vecs)
    while mats.shape[-3] > 1:
        mats, vecs = pair_up(mats, vecs, backward)
    return mats[..., 0, :, :], vecs[..., 0, :]


def keep_only(mats, vecs, keep):
    eye = jnp.eye(mats.shape[-1], dtype=jnp.float32)
    mats = jnp.where(keep[:, None, None], mats, eye)
    vecs = jnp.where(keep[:, None], vecs, 0.0)
    return mats, vecs


def pack(mat, vec):
    return jnp.concatenate((mat, vec[None, :]), axis=0)


def group_level(mat, vec, axis, backward):
    gathered = lax.all_gather(pack(mat, vec), axis)
    mats, vecs = gathered[:, :-1], gathered[:, -1]
    me = lax.axis_index(axis)
    index = jnp.arange(mats.shape[0])
    keep = index > me if backward else index < me
    pm, pv = keep_only(mats, vecs, keep)
    both_m = jnp.stack((pm, mats), axis=0)
    both_v = jnp.stack((pv, vecs), axis=0)
    rm, rv = reduce_maps(both_m, both_v, backward)
    return (rm[0], rv[0]), (rm[1], rv[1])


def across(mat, vec, backward):
    (pm, pv), (gm, gv) = group_level(mat, vec, "inner", backward)
    gathered = lax.all_gather(pack(gm, gv), "outer")
    mats, vecs = gathered[:, :-1], gathered[:, -1]
    me = lax.axis_index("outer")
    index = jnp.arange(mats.shape[0])
    keep = index > me if backward else index < me
    om, ov = reduce_maps(*keep_only(mats, vecs, keep), backward)
    return mm(pm, om), mv(pm, ov) + pv


def on_device(observations, gains, smoother_gains, transition, observation_map, initial_mean):
    me = lax.axis_index(AXES)
    devices = lax.axis_size(AXES)
    mapped = mm(observation_map, transition)
    forward_maps = transition[None] - jnp.einsum(
        "tij,jk->tik", gains, mapped, precision=exact, preferred_element_type=jnp.float32
    )
    forward_inputs = mv_whole(gains, observations)
    forward = local_tiers(forward_maps, forward_inputs, False)
    fm, fv = forward[-1][0][0], forward[-1][1][0]
    before_m, before_v = across(fm, fv, False)
    entry_state = mv(before_m, initial_mean) + before_v
    filtered = spread(forward, entry_state, False)

    predicted_all = jnp.dot(
        filtered, transition.T, precision=exact, preferred_element_type=jnp.float32
    )
    offsets = filtered - mv_whole(smoother_gains, predicted_all)
    backward = local_tiers(smoother_gains, offsets, True)
    bm, bv = backward[-1][0][0], backward[-1][1][0]
    last = me == devices - 1
    extra = jnp.where(last, predicted_all[-1], 0.0)
    bv = bv + mv(bm, extra)
    after_m, after_v = across(bm, bv, True)
    after_state = after_v + extra
    smoothed = spread(backward, after_state, True)
    return (filtered, smoothed)


def solution(mesh):
    in_specs = (
        P(AXES, None),
        P(AXES, None, None),
        P(AXES, None, None),
        P(),
        P(),
        P(),
    )
    out_specs = (P(AXES, None), P(AXES, None))
    return jax.shard_map(
        on_device, mesh=mesh, in_specs=in_specs, out_specs=out_specs, check_vma=False
    )
```

```python
import jax
import jax.numpy as jnp
from jax import lax
from jax.sharding import PartitionSpec as P

exact = lax.Precision.HIGHEST
AXES = ("outer", "inner")


def mm(a, b):
    return jnp.matmul(a, b, precision=exact, preferred_element_type=jnp.float32)


def mv(a, v):
    return jnp.einsum("...ij,...j->...i", a, v, precision=exact, preferred_element_type=jnp.float32)


def mv_whole(a, v):
    return jnp.sum(a * v[..., None, :], axis=-1)


def local_pair(mats, vecs, backward):
    count, width = mats.shape[0], mats.shape[-1]
    pm = mats.reshape(count // 2, 2, width, width)
    pv = vecs.reshape(count // 2, 2, width)
    first, second = (1, 0) if backward else (0, 1)
    joined = mm(pm[:, second], pm[:, first])
    partner = jnp.stack((pv[:, 1], pv[:, 0]), axis=1).reshape(count, width)
    crossed = mv_whole(mats, partner).reshape(count // 2, 2, width)
    return joined, crossed[:, second] + pv[:, second]


def pair_up(mats, vecs, backward):
    shape = mats.shape
    pm = mats.reshape(shape[:-3] + (shape[-3] // 2, 2) + shape[-2:])
    pv = vecs.reshape(vecs.shape[:-2] + (vecs.shape[-2] // 2, 2, vecs.shape[-1]))
    first, second = (1, 0) if backward else (0, 1)
    m1, m2 = pm[..., first, :, :], pm[..., second, :, :]
    v1, v2 = pv[..., first, :], pv[..., second, :]
    return mm(m2, m1), mv(m2, v1) + v2


def local_tiers(mats, vecs, backward):
    tiers = [(mats, vecs)]
    while tiers[-1][0].shape[0] > 1:
        tiers.append(local_pair(tiers[-1][0], tiers[-1][1], backward))
    return tiers


def spread(tiers, entry, backward):
    width = entry.shape[0]
    states = entry[None, :]
    for height in reversed(range(len(tiers) - 1)):
        mats, vecs = tiers[height]
        half = mats.shape[0] // 2
        pv = vecs.reshape(half, 2, width)
        both = jnp.broadcast_to(states[:, None, :], (half, 2, width)).reshape(-1, width)
        applied = mv_whole(mats, both).reshape(half, 2, width)
        if backward:
            other = applied[:, 1] + pv[:, 1]
            states = jnp.stack((other, states), axis=1)
        else:
            other = applied[:, 0] + pv[:, 0]
            states = jnp.stack((states, other), axis=1)
        states = states.reshape(-1, width)
    return mv_whole(tiers[0][0], states) + tiers[0][1]


def pad_pow2(mats, vecs):
    count = mats.shape[-3]
    size = 1
    while size < count:
        size *= 2
    if size > count:
        width = mats.shape[-1]
        eye = jnp.broadcast_to(
            jnp.eye(width, dtype=mats.dtype), mats.shape[:-3] + (size - count, width, width)
        )
        mats = jnp.concatenate((mats, eye), axis=-3)
        zero = jnp.zeros(vecs.shape[:-2] + (size - count, width), vecs.dtype)
        vecs = jnp.concatenate((vecs, zero), axis=-2)
    return mats, vecs


def reduce_maps(mats, vecs, backward):
    mats, vecs = pad_pow2(mats, vecs)
    while mats.shape[-3] > 1:
        mats, vecs = pair_up(mats, vecs, backward)
    return mats[..., 0, :, :], vecs[..., 0, :]


def keep_only(mats, vecs, keep):
    eye = jnp.eye(mats.shape[-1], dtype=jnp.float32)
    mats = jnp.where(keep[:, None, None], mats, eye)
    vecs = jnp.where(keep[:, None], vecs, 0.0)
    return mats, vecs


def pack(mat, vec):
    return jnp.concatenate((mat, vec[None, :]), axis=0)


def group_level(mat, vec, axis, backward):
    gathered = lax.all_gather(pack(mat, vec), axis)
    mats, vecs = gathered[:, :-1], gathered[:, -1]
    me = lax.axis_index(axis)
    index = jnp.arange(mats.shape[0])
    keep = index > me if backward else index < me
    pm, pv = keep_only(mats, vecs, keep)
    both_m = jnp.stack((pm, mats), axis=0)
    both_v = jnp.stack((pv, vecs), axis=0)
    rm, rv = reduce_maps(both_m, both_v, backward)
    return (rm[0], rv[0]), (rm[1], rv[1])


def from_other_groups(packed, backward):
    count = lax.axis_size("outer")
    me = lax.axis_index("outer")
    received = []
    keep = []
    for shift in reversed(range(1, count)):
        step = -shift if backward else shift
        pairs = [(i, (i + step) % count) for i in range(count)]
        received.append(lax.ppermute(packed, "outer", pairs))
        keep.append(me + shift <= count - 1 if backward else me - shift >= 0)
    if not received:
        return None
    maps = jnp.stack(received)
    return keep_only(maps[:, :-1], maps[:, -1], jnp.stack(keep))


def across(mat, vec, backward):
    (pm, pv), (gm, gv) = group_level(mat, vec, "inner", backward)
    others = from_other_groups(pack(gm, gv), backward)
    if others is None:
        return pm, pv
    om, ov = reduce_maps(others[0], others[1], False)
    return mm(pm, om), mv(pm, ov) + pv


def on_device(observations, gains, smoother_gains, transition, observation_map, initial_mean):
    me = lax.axis_index(AXES)
    devices = lax.axis_size(AXES)
    mapped = mm(observation_map, transition)
    forward_maps = transition[None] - jnp.einsum(
        "tij,jk->tik", gains, mapped, precision=exact, preferred_element_type=jnp.float32
    )
    forward_inputs = mv_whole(gains, observations)
    forward = local_tiers(forward_maps, forward_inputs, False)
    fm, fv = forward[-1][0][0], forward[-1][1][0]
    before_m, before_v = across(fm, fv, False)
    entry_state = mv(before_m, initial_mean) + before_v
    filtered = spread(forward, entry_state, False)

    predicted_all = jnp.dot(
        filtered, transition.T, precision=exact, preferred_element_type=jnp.float32
    )
    offsets = filtered - mv_whole(smoother_gains, predicted_all)
    backward = local_tiers(smoother_gains, offsets, True)
    bm, bv = backward[-1][0][0], backward[-1][1][0]
    last = me == devices - 1
    extra = jnp.where(last, predicted_all[-1], 0.0)
    bv = bv + mv(bm, extra)
    after_m, after_v = across(bm, bv, True)
    after_state = after_v + extra
    smoothed = spread(backward, after_state, True)
    return (filtered, smoothed)


def solution(mesh):
    in_specs = (
        P(AXES, None),
        P(AXES, None, None),
        P(AXES, None, None),
        P(),
        P(),
        P(),
    )
    out_specs = (P(AXES, None), P(AXES, None))
    return jax.shard_map(
        on_device, mesh=mesh, in_specs=in_specs, out_specs=out_specs, check_vma=False
    )
```

```python
import jax
import jax.numpy as jnp
from jax import lax
from jax.sharding import PartitionSpec as P

exact = lax.Precision.HIGHEST
AXES = ("outer", "inner")


def mm(a, b):
    return jnp.matmul(a, b, precision=exact, preferred_element_type=jnp.float32)


def mv(a, v):
    return jnp.einsum("...ij,...j->...i", a, v, precision=exact, preferred_element_type=jnp.float32)


def mv_whole(a, v):
    return jnp.sum(a * v[..., None, :], axis=-1)


def local_pair(mats, vecs, backward):
    count, width = mats.shape[0], mats.shape[-1]
    pm = mats.reshape(count // 2, 2, width, width)
    pv = vecs.reshape(count // 2, 2, width)
    first, second = (1, 0) if backward else (0, 1)
    joined = mm(pm[:, second], pm[:, first])
    partner = jnp.stack((pv[:, 1], pv[:, 0]), axis=1).reshape(count, width)
    crossed = mv_whole(mats, partner).reshape(count // 2, 2, width)
    return joined, crossed[:, second] + pv[:, second]


def pair_up(mats, vecs, backward):
    shape = mats.shape
    pm = mats.reshape(shape[:-3] + (shape[-3] // 2, 2) + shape[-2:])
    pv = vecs.reshape(vecs.shape[:-2] + (vecs.shape[-2] // 2, 2, vecs.shape[-1]))
    first, second = (1, 0) if backward else (0, 1)
    m1, m2 = pm[..., first, :, :], pm[..., second, :, :]
    v1, v2 = pv[..., first, :], pv[..., second, :]
    return mm(m2, m1), mv(m2, v1) + v2


def local_tiers(mats, vecs, backward):
    tiers = [(mats, vecs)]
    while tiers[-1][0].shape[0] > 1:
        tiers.append(local_pair(tiers[-1][0], tiers[-1][1], backward))
    return tiers


def matrix_tiers(mats, backward):
    tiers = [mats]
    width = mats.shape[-1]
    while tiers[-1].shape[0] > 1:
        below = tiers[-1]
        pm = below.reshape(below.shape[0] // 2, 2, width, width)
        first, second = (1, 0) if backward else (0, 1)
        tiers.append(mm(pm[:, second], pm[:, first]))
    return tiers


def vector_tiers(mats_tiers, vecs, backward):
    tiers = [(mats_tiers[0], vecs)]
    width = vecs.shape[-1]
    first, second = (1, 0) if backward else (0, 1)
    for mats, joined in zip(mats_tiers[:-1], mats_tiers[1:]):
        below = tiers[-1][1]
        count = below.shape[0]
        pv = below.reshape(count // 2, 2, width)
        partner = jnp.stack((pv[:, 1], pv[:, 0]), axis=1).reshape(count, width)
        crossed = mv_whole(mats, partner).reshape(count // 2, 2, width)
        tiers.append((joined, crossed[:, second] + pv[:, second]))
    return tiers


def spread(tiers, entry, backward):
    width = entry.shape[0]
    states = entry[None, :]
    for height in reversed(range(len(tiers) - 1)):
        mats, vecs = tiers[height]
        half = mats.shape[0] // 2
        pv = vecs.reshape(half, 2, width)
        both = jnp.broadcast_to(states[:, None, :], (half, 2, width)).reshape(-1, width)
        applied = mv_whole(mats, both).reshape(half, 2, width)
        if backward:
            other = applied[:, 1] + pv[:, 1]
            states = jnp.stack((other, states), axis=1)
        else:
            other = applied[:, 0] + pv[:, 0]
            states = jnp.stack((states, other), axis=1)
        states = states.reshape(-1, width)
    return mv_whole(tiers[0][0], states) + tiers[0][1]


def pad_pow2(mats, vecs):
    count = mats.shape[-3]
    size = 1
    while size < count:
        size *= 2
    if size > count:
        width = mats.shape[-1]
        eye = jnp.broadcast_to(
            jnp.eye(width, dtype=mats.dtype), mats.shape[:-3] + (size - count, width, width)
        )
        mats = jnp.concatenate((mats, eye), axis=-3)
        zero = jnp.zeros(vecs.shape[:-2] + (size - count, width), vecs.dtype)
        vecs = jnp.concatenate((vecs, zero), axis=-2)
    return mats, vecs


def reduce_maps(mats, vecs, backward):
    mats, vecs = pad_pow2(mats, vecs)
    while mats.shape[-3] > 1:
        mats, vecs = pair_up(mats, vecs, backward)
    return mats[..., 0, :, :], vecs[..., 0, :]


def keep_only(mats, vecs, keep):
    eye = jnp.eye(mats.shape[-1], dtype=jnp.float32)
    mats = jnp.where(keep[:, None, None], mats, eye)
    vecs = jnp.where(keep[:, None], vecs, 0.0)
    return mats, vecs


def pack(mat, vec):
    return jnp.concatenate((mat, vec[None, :]), axis=0)


def group_level(mat, vec, axis, backward):
    gathered = lax.all_gather(pack(mat, vec), axis)
    mats, vecs = gathered[:, :-1], gathered[:, -1]
    me = lax.axis_index(axis)
    index = jnp.arange(mats.shape[0])
    keep = index > me if backward else index < me
    pm, pv = keep_only(mats, vecs, keep)
    both_m = jnp.stack((pm, mats), axis=0)
    both_v = jnp.stack((pv, vecs), axis=0)
    rm, rv = reduce_maps(both_m, both_v, backward)
    return (rm[0], rv[0]), (rm[1], rv[1])


def from_other_groups(packed, backward):
    count = lax.axis_size("outer")
    me = lax.axis_index("outer")
    received = []
    keep = []
    for shift in reversed(range(1, count)):
        step = -shift if backward else shift
        pairs = [(i, (i + step) % count) for i in range(count)]
        received.append(lax.ppermute(packed, "outer", pairs))
        keep.append(me + shift <= count - 1 if backward else me - shift >= 0)
    if not received:
        return None
    maps = jnp.stack(received)
    return keep_only(maps[:, :-1], maps[:, -1], jnp.stack(keep))


def across(mat, vec, backward):
    (pm, pv), (gm, gv) = group_level(mat, vec, "inner", backward)
    others = from_other_groups(pack(gm, gv), backward)
    if others is None:
        return pm, pv
    om, ov = reduce_maps(others[0], others[1], False)
    return mm(pm, om), mv(pm, ov) + pv


def on_device(observations, gains, smoother_gains, transition, observation_map, initial_mean):
    me = lax.axis_index(AXES)
    devices = lax.axis_size(AXES)
    back_mats = lax.optimization_barrier(matrix_tiers(smoother_gains, True))
    mapped = mm(observation_map, transition)
    forward_maps = transition[None] - jnp.einsum(
        "tij,jk->tik", gains, mapped, precision=exact, preferred_element_type=jnp.float32
    )
    forward_inputs = mv_whole(gains, observations)
    forward = local_tiers(forward_maps, forward_inputs, False)
    fm, fv = forward[-1][0][0], forward[-1][1][0]
    before_m, before_v = across(fm, fv, False)
    entry_state = mv(before_m, initial_mean) + before_v
    filtered = spread(forward, entry_state, False)

    predicted_all = jnp.dot(
        filtered, transition.T, precision=exact, preferred_element_type=jnp.float32
    )
    offsets = filtered - mv_whole(smoother_gains, predicted_all)
    backward = vector_tiers(back_mats, offsets, True)
    bm, bv = backward[-1][0][0], backward[-1][1][0]
    last = me == devices - 1
    extra = jnp.where(last, predicted_all[-1], 0.0)
    bv = bv + mv(bm, extra)
    after_m, after_v = across(bm, bv, True)
    after_state = after_v + extra
    smoothed = spread(backward, after_state, True)
    return (filtered, smoothed)


def solution(mesh):
    in_specs = (
        P(AXES, None),
        P(AXES, None, None),
        P(AXES, None, None),
        P(),
        P(),
        P(),
    )
    out_specs = (P(AXES, None), P(AXES, None))
    return jax.shard_map(
        on_device, mesh=mesh, in_specs=in_specs, out_specs=out_specs, check_vma=False
    )
```

```python
import jax
import jax.numpy as jnp
from jax import lax
from jax.sharding import PartitionSpec as P

exact = lax.Precision.HIGHEST
AXES = ("outer", "inner")


def mm(a, b):
    return jnp.matmul(a, b, precision=exact, preferred_element_type=jnp.float32)


def mv(a, v):
    return jnp.einsum("...ij,...j->...i", a, v, precision=exact, preferred_element_type=jnp.float32)


def mv_whole(a, v):
    return jnp.sum(a * v[..., None, :], axis=-1)


def local_pair(mats, vecs, backward):
    count, width = mats.shape[0], mats.shape[-1]
    pm = mats.reshape(count // 2, 2, width, width)
    pv = vecs.reshape(count // 2, 2, width)
    first, second = (1, 0) if backward else (0, 1)
    joined = mm(pm[:, second], pm[:, first])
    partner = jnp.stack((pv[:, 1], pv[:, 0]), axis=1).reshape(count, width)
    crossed = mv_whole(mats, partner).reshape(count // 2, 2, width)
    return joined, crossed[:, second] + pv[:, second]


def pair_up(mats, vecs, backward):
    shape = mats.shape
    pm = mats.reshape(shape[:-3] + (shape[-3] // 2, 2) + shape[-2:])
    pv = vecs.reshape(vecs.shape[:-2] + (vecs.shape[-2] // 2, 2, vecs.shape[-1]))
    first, second = (1, 0) if backward else (0, 1)
    m1, m2 = pm[..., first, :, :], pm[..., second, :, :]
    v1, v2 = pv[..., first, :], pv[..., second, :]
    return mm(m2, m1), mv(m2, v1) + v2


def local_tiers(mats, vecs, backward):
    tiers = [(mats, vecs)]
    while tiers[-1][0].shape[0] > 1:
        tiers.append(local_pair(tiers[-1][0], tiers[-1][1], backward))
    return tiers


def spread(tiers, entry, backward):
    width = entry.shape[0]
    states = entry[None, :]
    for height in reversed(range(len(tiers) - 1)):
        mats, vecs = tiers[height]
        half = mats.shape[0] // 2
        pv = vecs.reshape(half, 2, width)
        both = jnp.broadcast_to(states[:, None, :], (half, 2, width)).reshape(-1, width)
        applied = mv_whole(mats, both).reshape(half, 2, width)
        if backward:
            other = applied[:, 1] + pv[:, 1]
            states = jnp.stack((other, states), axis=1)
        else:
            other = applied[:, 0] + pv[:, 0]
            states = jnp.stack((states, other), axis=1)
        states = states.reshape(-1, width)
    return mv_whole(tiers[0][0], states) + tiers[0][1]


def pad_pow2(mats, vecs):
    count = mats.shape[-3]
    size = 1
    while size < count:
        size *= 2
    if size > count:
        width = mats.shape[-1]
        eye = jnp.broadcast_to(
            jnp.eye(width, dtype=mats.dtype), mats.shape[:-3] + (size - count, width, width)
        )
        mats = jnp.concatenate((mats, eye), axis=-3)
        zero = jnp.zeros(vecs.shape[:-2] + (size - count, width), vecs.dtype)
        vecs = jnp.concatenate((vecs, zero), axis=-2)
    return mats, vecs


def reduce_maps(mats, vecs, backward):
    mats, vecs = pad_pow2(mats, vecs)
    while mats.shape[-3] > 1:
        mats, vecs = pair_up(mats, vecs, backward)
    return mats[..., 0, :, :], vecs[..., 0, :]


def keep_only(mats, vecs, keep):
    eye = jnp.eye(mats.shape[-1], dtype=jnp.float32)
    mats = jnp.where(keep[:, None, None], mats, eye)
    vecs = jnp.where(keep[:, None], vecs, 0.0)
    return mats, vecs


def pack(mat, vec):
    return jnp.concatenate((mat, vec[None, :]), axis=0)


def from_other_groups(packed, backward):
    count = lax.axis_size("outer")
    me = lax.axis_index("outer")
    received = []
    keep = []
    for shift in reversed(range(1, count)):
        step = -shift if backward else shift
        pairs = [(i, (i + step) % count) for i in range(count)]
        received.append(lax.ppermute(packed, "outer", pairs))
        keep.append(me + shift <= count - 1 if backward else me - shift >= 0)
    return received, keep


def across(mat, vec, start, backward):
    gathered = lax.all_gather(pack(mat, vec), "inner")
    mats, vecs = gathered[:, :-1], gathered[:, -1]
    gm, gv = reduce_maps(mats, vecs, backward)
    received, keep = from_other_groups(pack(gm, gv), backward)
    me = lax.axis_index("inner")
    index = jnp.arange(mats.shape[0])
    mine = index > me if backward else index < me
    pm, pv = reduce_maps(*keep_only(mats, vecs, mine), backward)
    state = start
    for block, kept in zip(received, keep):
        moved = mv_whole(block[:-1], state) + block[-1]
        state = jnp.where(kept, moved, state)
    return mv_whole(pm, state) + pv


def on_device(observations, gains, smoother_gains, transition, observation_map, initial_mean):
    me = lax.axis_index(AXES)
    devices = lax.axis_size(AXES)
    mapped = mm(observation_map, transition)
    forward_maps = transition[None] - jnp.einsum(
        "tij,jk->tik", gains, mapped, precision=exact, preferred_element_type=jnp.float32
    )
    forward_inputs = mv_whole(gains, observations)
    forward = local_tiers(forward_maps, forward_inputs, False)
    fm, fv = forward[-1][0][0], forward[-1][1][0]
    entry_state = across(fm, fv, initial_mean, False)
    filtered = spread(forward, entry_state, False)

    predicted_all = jnp.dot(
        filtered, transition.T, precision=exact, preferred_element_type=jnp.float32
    )
    offsets = filtered - mv_whole(smoother_gains, predicted_all)
    backward = local_tiers(smoother_gains, offsets, True)
    bm, bv = backward[-1][0][0], backward[-1][1][0]
    last = me == devices - 1
    extra = jnp.where(last, predicted_all[-1], 0.0)
    bv = bv + mv(bm, extra)
    after_state = across(bm, bv, jnp.zeros_like(extra), True) + extra
    smoothed = spread(backward, after_state, True)
    return (filtered, smoothed)


def solution(mesh):
    in_specs = (
        P(AXES, None),
        P(AXES, None, None),
        P(AXES, None, None),
        P(),
        P(),
        P(),
    )
    out_specs = (P(AXES, None), P(AXES, None))
    return jax.shard_map(
        on_device, mesh=mesh, in_specs=in_specs, out_specs=out_specs, check_vma=False
    )
```

```python
import jax
import jax.numpy as jnp
from jax import lax
from jax.sharding import PartitionSpec as P

exact = lax.Precision.HIGHEST
AXES = ("outer", "inner")


def mm(a, b):
    return jnp.matmul(a, b, precision=exact, preferred_element_type=jnp.float32)


def mv(a, v):
    return jnp.einsum("...ij,...j->...i", a, v, precision=exact, preferred_element_type=jnp.float32)


def mv_whole(a, v):
    return jnp.sum(a * v[..., None, :], axis=-1)


def local_pair(mats, vecs, backward):
    count, width = mats.shape[0], mats.shape[-1]
    pm = mats.reshape(count // 2, 2, width, width)
    pv = vecs.reshape(count // 2, 2, width)
    first, second = (1, 0) if backward else (0, 1)
    joined = mm(pm[:, second], pm[:, first])
    partner = jnp.stack((pv[:, 1], pv[:, 0]), axis=1).reshape(count, width)
    crossed = mv_whole(mats, partner).reshape(count // 2, 2, width)
    return joined, crossed[:, second] + pv[:, second]


def pair_up(mats, vecs, backward):
    shape = mats.shape
    pm = mats.reshape(shape[:-3] + (shape[-3] // 2, 2) + shape[-2:])
    pv = vecs.reshape(vecs.shape[:-2] + (vecs.shape[-2] // 2, 2, vecs.shape[-1]))
    first, second = (1, 0) if backward else (0, 1)
    m1, m2 = pm[..., first, :, :], pm[..., second, :, :]
    v1, v2 = pv[..., first, :], pv[..., second, :]
    return mm(m2, m1), mv(m2, v1) + v2


def local_tiers(mats, vecs, backward):
    tiers = [(mats, vecs)]
    while tiers[-1][0].shape[0] > 1:
        tiers.append(local_pair(tiers[-1][0], tiers[-1][1], backward))
    return tiers


def spread(tiers, entry, backward):
    width = entry.shape[0]
    states = entry[None, :]
    for height in reversed(range(len(tiers) - 1)):
        mats, vecs = tiers[height]
        half = mats.shape[0] // 2
        pv = vecs.reshape(half, 2, width)
        both = jnp.broadcast_to(states[:, None, :], (half, 2, width)).reshape(-1, width)
        applied = mv_whole(mats, both).reshape(half, 2, width)
        if backward:
            other = applied[:, 1] + pv[:, 1]
            states = jnp.stack((other, states), axis=1)
        else:
            other = applied[:, 0] + pv[:, 0]
            states = jnp.stack((states, other), axis=1)
        states = states.reshape(-1, width)
    return mv_whole(tiers[0][0], states) + tiers[0][1]


def pad_pow2(mats, vecs):
    count = mats.shape[-3]
    size = 1
    while size < count:
        size *= 2
    if size > count:
        width = mats.shape[-1]
        eye = jnp.broadcast_to(
            jnp.eye(width, dtype=mats.dtype), mats.shape[:-3] + (size - count, width, width)
        )
        mats = jnp.concatenate((mats, eye), axis=-3)
        zero = jnp.zeros(vecs.shape[:-2] + (size - count, width), vecs.dtype)
        vecs = jnp.concatenate((vecs, zero), axis=-2)
    return mats, vecs


def reduce_maps(mats, vecs, backward):
    mats, vecs = pad_pow2(mats, vecs)
    while mats.shape[-3] > 1:
        mats, vecs = pair_up(mats, vecs, backward)
    return mats[..., 0, :, :], vecs[..., 0, :]


def keep_only(mats, vecs, keep):
    eye = jnp.eye(mats.shape[-1], dtype=jnp.float32)
    mats = jnp.where(keep[:, None, None], mats, eye)
    vecs = jnp.where(keep[:, None], vecs, 0.0)
    return mats, vecs


def pack(mat, vec):
    return jnp.concatenate((mat, vec[None, :]), axis=0)


def from_other_groups(packed, backward):
    count = lax.axis_size("outer")
    me = lax.axis_index("outer")
    received = []
    keep = []
    for shift in reversed(range(1, count)):
        step = -shift if backward else shift
        pairs = [(i, i + step) for i in range(count) if 0 <= i + step < count]
        received.append(lax.ppermute(packed, "outer", pairs))
        keep.append(me + shift <= count - 1 if backward else me - shift >= 0)
    return received, keep


def across(mat, vec, start, backward):
    gathered = lax.all_gather(pack(mat, vec), "inner")
    mats, vecs = gathered[:, :-1], gathered[:, -1]
    gm, gv = reduce_maps(mats, vecs, backward)
    received, keep = from_other_groups(pack(gm, gv), backward)
    me = lax.axis_index("inner")
    index = jnp.arange(mats.shape[0])
    mine = index > me if backward else index < me
    pm, pv = reduce_maps(*keep_only(mats, vecs, mine), backward)
    state = start
    for block, kept in zip(received, keep):
        moved = mv_whole(block[:-1], state) + block[-1]
        state = jnp.where(kept, moved, state)
    return mv_whole(pm, state) + pv


def on_device(observations, gains, smoother_gains, transition, observation_map, initial_mean):
    me = lax.axis_index(AXES)
    devices = lax.axis_size(AXES)
    mapped = mm(observation_map, transition)
    forward_maps = transition[None] - jnp.einsum(
        "tij,jk->tik", gains, mapped, precision=exact, preferred_element_type=jnp.float32
    )
    forward_inputs = mv_whole(gains, observations)
    forward = local_tiers(forward_maps, forward_inputs, False)
    fm, fv = forward[-1][0][0], forward[-1][1][0]
    entry_state = across(fm, fv, initial_mean, False)
    filtered = spread(forward, entry_state, False)

    predicted_all = jnp.dot(
        filtered, transition.T, precision=exact, preferred_element_type=jnp.float32
    )
    offsets = filtered - mv_whole(smoother_gains, predicted_all)
    backward = local_tiers(smoother_gains, offsets, True)
    bm, bv = backward[-1][0][0], backward[-1][1][0]
    last = me == devices - 1
    extra = jnp.where(last, predicted_all[-1], 0.0)
    bv = bv + mv(bm, extra)
    after_state = across(bm, bv, jnp.zeros_like(extra), True) + extra
    smoothed = spread(backward, after_state, True)
    return (filtered, smoothed)


def solution(mesh):
    in_specs = (
        P(AXES, None),
        P(AXES, None, None),
        P(AXES, None, None),
        P(),
        P(),
        P(),
    )
    out_specs = (P(AXES, None), P(AXES, None))
    return jax.shard_map(
        on_device, mesh=mesh, in_specs=in_specs, out_specs=out_specs, check_vma=False
    )
```

```python
import jax
import jax.numpy as jnp
from jax import lax
from jax.sharding import PartitionSpec as P

exact = lax.Precision.HIGHEST
AXES = ("outer", "inner")


def mm(a, b):
    return jnp.matmul(a, b, precision=exact, preferred_element_type=jnp.float32)


def mv(a, v):
    return jnp.einsum("...ij,...j->...i", a, v, precision=exact, preferred_element_type=jnp.float32)


def mv_whole(a, v):
    return jnp.sum(a * v[..., None, :], axis=-1)


def local_pair(mats, vecs, backward):
    count, width = mats.shape[0], mats.shape[-1]
    pm = mats.reshape(count // 2, 2, width, width)
    pv = vecs.reshape(count // 2, 2, width)
    first, second = (1, 0) if backward else (0, 1)
    joined = mm(pm[:, second], pm[:, first])
    partner = jnp.stack((pv[:, 1], pv[:, 0]), axis=1).reshape(count, width)
    crossed = mv_whole(mats, partner).reshape(count // 2, 2, width)
    return joined, crossed[:, second] + pv[:, second]


def pair_up(mats, vecs, backward):
    shape = mats.shape
    pm = mats.reshape(shape[:-3] + (shape[-3] // 2, 2) + shape[-2:])
    pv = vecs.reshape(vecs.shape[:-2] + (vecs.shape[-2] // 2, 2, vecs.shape[-1]))
    first, second = (1, 0) if backward else (0, 1)
    m1, m2 = pm[..., first, :, :], pm[..., second, :, :]
    v1, v2 = pv[..., first, :], pv[..., second, :]
    return mm(m2, m1), mv(m2, v1) + v2


def local_tiers(mats, vecs, backward):
    tiers = [(mats, vecs)]
    while tiers[-1][0].shape[0] > 1:
        tiers.append(local_pair(tiers[-1][0], tiers[-1][1], backward))
    return tiers


def spread(tiers, entry, backward):
    width = entry.shape[0]
    states = entry[None, :]
    for height in reversed(range(len(tiers) - 1)):
        mats, vecs = tiers[height]
        half = mats.shape[0] // 2
        pv = vecs.reshape(half, 2, width)
        both = jnp.broadcast_to(states[:, None, :], (half, 2, width)).reshape(-1, width)
        applied = mv_whole(mats, both).reshape(half, 2, width)
        if backward:
            other = applied[:, 1] + pv[:, 1]
            states = jnp.stack((other, states), axis=1)
        else:
            other = applied[:, 0] + pv[:, 0]
            states = jnp.stack((states, other), axis=1)
        states = states.reshape(-1, width)
    return mv_whole(tiers[0][0], states) + tiers[0][1]


def pad_pow2(mats, vecs):
    count = mats.shape[-3]
    size = 1
    while size < count:
        size *= 2
    if size > count:
        width = mats.shape[-1]
        eye = jnp.broadcast_to(
            jnp.eye(width, dtype=mats.dtype), mats.shape[:-3] + (size - count, width, width)
        )
        mats = jnp.concatenate((mats, eye), axis=-3)
        zero = jnp.zeros(vecs.shape[:-2] + (size - count, width), vecs.dtype)
        vecs = jnp.concatenate((vecs, zero), axis=-2)
    return mats, vecs


def reduce_maps(mats, vecs, backward):
    mats, vecs = pad_pow2(mats, vecs)
    while mats.shape[-3] > 1:
        mats, vecs = local_pair(mats, vecs, backward)
    return mats[..., 0, :, :], vecs[..., 0, :]


def keep_only(mats, vecs, keep):
    eye = jnp.eye(mats.shape[-1], dtype=jnp.float32)
    mats = jnp.where(keep[:, None, None], mats, eye)
    vecs = jnp.where(keep[:, None], vecs, 0.0)
    return mats, vecs


def pack(mat, vec):
    return jnp.concatenate((mat, vec[None, :]), axis=0)


def from_other_groups(packed, backward):
    count = lax.axis_size("outer")
    me = lax.axis_index("outer")
    received = []
    keep = []
    for shift in reversed(range(1, count)):
        step = -shift if backward else shift
        pairs = [(i, (i + step) % count) for i in range(count)]
        received.append(lax.ppermute(packed, "outer", pairs))
        keep.append(me + shift <= count - 1 if backward else me - shift >= 0)
    return received, keep


def across(mat, vec, start, backward):
    gathered = lax.all_gather(pack(mat, vec), "inner")
    mats, vecs = gathered[:, :-1], gathered[:, -1]
    gm, gv = reduce_maps(mats, vecs, backward)
    received, keep = from_other_groups(pack(gm, gv), backward)
    me = lax.axis_index("inner")
    index = jnp.arange(mats.shape[0])
    mine = index > me if backward else index < me
    pm, pv = reduce_maps(*keep_only(mats, vecs, mine), backward)
    state = start
    for block, kept in zip(received, keep):
        moved = mv_whole(block[:-1], state) + block[-1]
        state = jnp.where(kept, moved, state)
    return mv_whole(pm, state) + pv


def on_device(observations, gains, smoother_gains, transition, observation_map, initial_mean):
    me = lax.axis_index(AXES)
    devices = lax.axis_size(AXES)
    mapped = mm(observation_map, transition)
    forward_maps = transition[None] - jnp.einsum(
        "tij,jk->tik", gains, mapped, precision=exact, preferred_element_type=jnp.float32
    )
    forward_inputs = mv_whole(gains, observations)
    forward = local_tiers(forward_maps, forward_inputs, False)
    fm, fv = forward[-1][0][0], forward[-1][1][0]
    entry_state = across(fm, fv, initial_mean, False)
    filtered = spread(forward, entry_state, False)

    predicted_all = jnp.dot(
        filtered, transition.T, precision=exact, preferred_element_type=jnp.float32
    )
    offsets = filtered - mv_whole(smoother_gains, predicted_all)
    backward = local_tiers(smoother_gains, offsets, True)
    bm, bv = backward[-1][0][0], backward[-1][1][0]
    last = me == devices - 1
    extra = jnp.where(last, predicted_all[-1], 0.0)
    bv = bv + mv_whole(bm, extra)
    after_state = across(bm, bv, jnp.zeros_like(extra), True) + extra
    smoothed = spread(backward, after_state, True)
    return (filtered, smoothed)


def solution(mesh):
    in_specs = (
        P(AXES, None),
        P(AXES, None, None),
        P(AXES, None, None),
        P(),
        P(),
        P(),
    )
    out_specs = (P(AXES, None), P(AXES, None))
    return jax.shard_map(
        on_device, mesh=mesh, in_specs=in_specs, out_specs=out_specs, check_vma=False
    )
```

```python
import jax
import jax.numpy as jnp
from jax import lax
from jax.sharding import PartitionSpec as P

exact = lax.Precision.HIGHEST
AXES = ("outer", "inner")


def mm(a, b):
    return jnp.matmul(a, b, precision=exact, preferred_element_type=jnp.float32)


def mv(a, v):
    return jnp.einsum("...ij,...j->...i", a, v, precision=exact, preferred_element_type=jnp.float32)


def mv_whole(a, v):
    return jnp.sum(a * v[..., None, :], axis=-1)


def local_pair(mats, vecs, backward):
    count, width = mats.shape[0], mats.shape[-1]
    pm = mats.reshape(count // 2, 2, width, width)
    pv = vecs.reshape(count // 2, 2, width)
    first, second = (1, 0) if backward else (0, 1)
    joined = mm(pm[:, second], pm[:, first])
    partner = jnp.stack((pv[:, 1], pv[:, 0]), axis=1).reshape(count, width)
    crossed = mv_whole(mats, partner).reshape(count // 2, 2, width)
    return joined, crossed[:, second] + pv[:, second]


def pair_up(mats, vecs, backward):
    shape = mats.shape
    pm = mats.reshape(shape[:-3] + (shape[-3] // 2, 2) + shape[-2:])
    pv = vecs.reshape(vecs.shape[:-2] + (vecs.shape[-2] // 2, 2, vecs.shape[-1]))
    first, second = (1, 0) if backward else (0, 1)
    m1, m2 = pm[..., first, :, :], pm[..., second, :, :]
    v1, v2 = pv[..., first, :], pv[..., second, :]
    return mm(m2, m1), mv(m2, v1) + v2


def local_tiers(mats, vecs, backward):
    tiers = [(mats, vecs)]
    while tiers[-1][0].shape[0] > 1:
        tiers.append(local_pair(tiers[-1][0], tiers[-1][1], backward))
    return tiers


def spread(tiers, entry, backward):
    width = entry.shape[0]
    states = entry[None, :]
    for height in reversed(range(len(tiers) - 1)):
        mats, vecs = tiers[height]
        half = mats.shape[0] // 2
        pv = vecs.reshape(half, 2, width)
        both = jnp.broadcast_to(states[:, None, :], (half, 2, width)).reshape(-1, width)
        applied = mv_whole(mats, both).reshape(half, 2, width)
        if backward:
            other = applied[:, 1] + pv[:, 1]
            states = jnp.stack((other, states), axis=1)
        else:
            other = applied[:, 0] + pv[:, 0]
            states = jnp.stack((states, other), axis=1)
        states = states.reshape(-1, width)
    return mv_whole(tiers[0][0], states) + tiers[0][1]


def pad_pow2(mats, vecs):
    count = mats.shape[-3]
    size = 1
    while size < count:
        size *= 2
    if size > count:
        width = mats.shape[-1]
        eye = jnp.broadcast_to(
            jnp.eye(width, dtype=mats.dtype), mats.shape[:-3] + (size - count, width, width)
        )
        mats = jnp.concatenate((mats, eye), axis=-3)
        zero = jnp.zeros(vecs.shape[:-2] + (size - count, width), vecs.dtype)
        vecs = jnp.concatenate((vecs, zero), axis=-2)
    return mats, vecs


def reduce_maps(mats, vecs, backward):
    mats, vecs = pad_pow2(mats, vecs)
    while mats.shape[-3] > 1:
        mats, vecs = local_pair(mats, vecs, backward)
    return mats[..., 0, :, :], vecs[..., 0, :]


def keep_only(mats, vecs, keep):
    eye = jnp.eye(mats.shape[-1], dtype=jnp.float32)
    mats = jnp.where(keep[:, None, None], mats, eye)
    vecs = jnp.where(keep[:, None], vecs, 0.0)
    return mats, vecs


def pack(mat, vec):
    return jnp.concatenate((mat, vec[None, :]), axis=0)


def from_other_groups(packed, backward):
    count = lax.axis_size("outer")
    me = lax.axis_index("outer")
    received = []
    keep = []
    for shift in reversed(range(1, count)):
        step = -shift if backward else shift
        pairs = [(i, (i + step) % count) for i in range(count)]
        received.append(lax.ppermute(packed, "outer", pairs))
        keep.append(me + shift <= count - 1 if backward else me - shift >= 0)
    return received, keep


def across(mat, vec, start, backward):
    gathered = lax.all_gather(pack(mat, vec), "inner")
    mats, vecs = gathered[:, :-1], gathered[:, -1]
    gm, gv = reduce_maps(mats, vecs, backward)
    received, keep = from_other_groups(pack(gm, gv), backward)
    me = lax.axis_index("inner")
    index = jnp.arange(mats.shape[0])
    mine = index > me if backward else index < me
    pm, pv = reduce_maps(*keep_only(mats, vecs, mine), backward)
    eye = jnp.eye(mat.shape[-1], dtype=jnp.float32)
    state = start
    for block, kept in zip(received, keep):
        state = mv_whole(jnp.where(kept, block[:-1], eye), state) + jnp.where(kept, block[-1], 0.0)
    return mv_whole(pm, state) + pv


def on_device(observations, gains, smoother_gains, transition, observation_map, initial_mean):
    me = lax.axis_index(AXES)
    devices = lax.axis_size(AXES)
    mapped = mm(observation_map, transition)
    forward_maps = transition[None] - jnp.einsum(
        "tij,jk->tik", gains, mapped, precision=exact, preferred_element_type=jnp.float32
    )
    forward_inputs = mv_whole(gains, observations)
    forward = local_tiers(forward_maps, forward_inputs, False)
    fm, fv = forward[-1][0][0], forward[-1][1][0]
    entry_state = across(fm, fv, initial_mean, False)
    filtered = spread(forward, entry_state, False)

    predicted_all = jnp.dot(
        filtered, transition.T, precision=exact, preferred_element_type=jnp.float32
    )
    offsets = filtered - mv_whole(smoother_gains, predicted_all)
    backward = local_tiers(smoother_gains, offsets, True)
    bm, bv = backward[-1][0][0], backward[-1][1][0]
    last = me == devices - 1
    extra = jnp.where(last, predicted_all[-1], 0.0)
    bv = bv + mv_whole(bm, extra)
    after_state = across(bm, bv, jnp.zeros_like(extra), True) + extra
    smoothed = spread(backward, after_state, True)
    return (filtered, smoothed)


def solution(mesh):
    in_specs = (
        P(AXES, None),
        P(AXES, None, None),
        P(AXES, None, None),
        P(),
        P(),
        P(),
    )
    out_specs = (P(AXES, None), P(AXES, None))
    return jax.shard_map(
        on_device, mesh=mesh, in_specs=in_specs, out_specs=out_specs, check_vma=False
    )
```

```python
import jax
import jax.numpy as jnp
from jax import lax
from jax.sharding import PartitionSpec as P

exact = lax.Precision.HIGHEST
AXES = ("outer", "inner")


def mm(a, b):
    return jnp.matmul(a, b, precision=exact, preferred_element_type=jnp.float32)


def mv(a, v):
    return jnp.einsum("...ij,...j->...i", a, v, precision=exact, preferred_element_type=jnp.float32)


def mv_whole(a, v):
    return jnp.sum(a * v[..., None, :], axis=-1)


def local_pair(mats, vecs, backward):
    count, width = mats.shape[0], mats.shape[-1]
    pm = mats.reshape(count // 2, 2, width, width)
    pv = vecs.reshape(count // 2, 2, width)
    first, second = (1, 0) if backward else (0, 1)
    joined = mm(pm[:, second], pm[:, first])
    partner = jnp.stack((pv[:, 1], pv[:, 0]), axis=1).reshape(count, width)
    crossed = mv_whole(mats, partner).reshape(count // 2, 2, width)
    return joined, crossed[:, second] + pv[:, second]


def pair_up(mats, vecs, backward):
    shape = mats.shape
    pm = mats.reshape(shape[:-3] + (shape[-3] // 2, 2) + shape[-2:])
    pv = vecs.reshape(vecs.shape[:-2] + (vecs.shape[-2] // 2, 2, vecs.shape[-1]))
    first, second = (1, 0) if backward else (0, 1)
    m1, m2 = pm[..., first, :, :], pm[..., second, :, :]
    v1, v2 = pv[..., first, :], pv[..., second, :]
    return mm(m2, m1), mv(m2, v1) + v2


def local_tiers(mats, vecs, backward):
    tiers = [(mats, vecs)]
    while tiers[-1][0].shape[0] > 1:
        tiers.append(local_pair(tiers[-1][0], tiers[-1][1], backward))
    return tiers


def spread(tiers, entry, backward):
    width = entry.shape[0]
    states = entry[None, :]
    for height in reversed(range(len(tiers) - 1)):
        mats, vecs = tiers[height]
        half = mats.shape[0] // 2
        pv = vecs.reshape(half, 2, width)
        both = jnp.broadcast_to(states[:, None, :], (half, 2, width)).reshape(-1, width)
        applied = mv_whole(mats, both).reshape(half, 2, width)
        if backward:
            other = applied[:, 1] + pv[:, 1]
            states = jnp.stack((other, states), axis=1)
        else:
            other = applied[:, 0] + pv[:, 0]
            states = jnp.stack((states, other), axis=1)
        states = states.reshape(-1, width)
    return mv_whole(tiers[0][0], states) + tiers[0][1]


def pad_pow2(mats, vecs):
    count = mats.shape[-3]
    size = 1
    while size < count:
        size *= 2
    if size > count:
        width = mats.shape[-1]
        eye = jnp.broadcast_to(
            jnp.eye(width, dtype=mats.dtype), mats.shape[:-3] + (size - count, width, width)
        )
        mats = jnp.concatenate((mats, eye), axis=-3)
        zero = jnp.zeros(vecs.shape[:-2] + (size - count, width), vecs.dtype)
        vecs = jnp.concatenate((vecs, zero), axis=-2)
    return mats, vecs


def reduce_maps(mats, vecs, backward):
    mats, vecs = pad_pow2(mats, vecs)
    while mats.shape[-3] > 1:
        mats, vecs = local_pair(mats, vecs, backward)
    return mats[..., 0, :, :], vecs[..., 0, :]


def keep_only(mats, vecs, keep):
    eye = jnp.eye(mats.shape[-1], dtype=jnp.float32)
    mats = jnp.where(keep[:, None, None], mats, eye)
    vecs = jnp.where(keep[:, None], vecs, 0.0)
    return mats, vecs


def pack(mat, vec):
    return jnp.concatenate((mat, vec[None, :]), axis=0)


def from_other_groups(packed, backward):
    count = lax.axis_size("outer")
    me = lax.axis_index("outer")
    received = []
    keep = []
    for shift in reversed(range(1, count)):
        step = -shift if backward else shift
        pairs = [(i, (i + step) % count) for i in range(count)]
        received.append(lax.ppermute(packed, "outer", pairs))
        keep.append(me + shift <= count - 1 if backward else me - shift >= 0)
    return received, keep


def across(mat, vec, start, backward):
    gathered = lax.all_gather(pack(mat, vec), "inner")
    mats, vecs = gathered[:, :-1], gathered[:, -1]
    gm, gv = reduce_maps(mats, vecs, backward)
    received, keep = from_other_groups(pack(gm, gv), backward)
    me = lax.axis_index("inner")
    index = jnp.arange(mats.shape[0])
    mine = index > me if backward else index < me
    pm, pv = reduce_maps(*keep_only(mats, vecs, mine), backward)
    eye = jnp.eye(mat.shape[-1], dtype=jnp.float32)
    state = start
    for block, kept in zip(received, keep):
        mat = jnp.where(kept, block[:-1], eye)
        shift = jnp.where(kept, block[-1], 0.0) / mat.shape[-1]
        state = jnp.sum(mat * state[None, :] + shift[:, None], axis=-1)
    return mv_whole(pm, state) + pv


def on_device(observations, gains, smoother_gains, transition, observation_map, initial_mean):
    me = lax.axis_index(AXES)
    devices = lax.axis_size(AXES)
    mapped = mm(observation_map, transition)
    forward_maps = transition[None] - jnp.einsum(
        "tij,jk->tik", gains, mapped, precision=exact, preferred_element_type=jnp.float32
    )
    forward_inputs = mv_whole(gains, observations)
    forward = local_tiers(forward_maps, forward_inputs, False)
    fm, fv = forward[-1][0][0], forward[-1][1][0]
    entry_state = across(fm, fv, initial_mean, False)
    filtered = spread(forward, entry_state, False)

    predicted_all = jnp.dot(
        filtered, transition.T, precision=exact, preferred_element_type=jnp.float32
    )
    offsets = filtered - mv_whole(smoother_gains, predicted_all)
    backward = local_tiers(smoother_gains, offsets, True)
    bm, bv = backward[-1][0][0], backward[-1][1][0]
    last = me == devices - 1
    extra = jnp.where(last, predicted_all[-1], 0.0)
    bv = bv + mv_whole(bm, extra)
    after_state = across(bm, bv, jnp.zeros_like(extra), True) + extra
    smoothed = spread(backward, after_state, True)
    return (filtered, smoothed)


def solution(mesh):
    in_specs = (
        P(AXES, None),
        P(AXES, None, None),
        P(AXES, None, None),
        P(),
        P(),
        P(),
    )
    out_specs = (P(AXES, None), P(AXES, None))
    return jax.shard_map(
        on_device, mesh=mesh, in_specs=in_specs, out_specs=out_specs, check_vma=False
    )
```

```python
import jax
import jax.numpy as jnp
from jax import lax
from jax.sharding import PartitionSpec as P

exact = lax.Precision.HIGHEST
AXES = ("outer", "inner")


def mm(a, b):
    return jnp.matmul(a, b, precision=exact, preferred_element_type=jnp.float32)


def mv(a, v):
    return jnp.einsum("...ij,...j->...i", a, v, precision=exact, preferred_element_type=jnp.float32)


def mv_whole(a, v):
    return jnp.sum(a * v[..., None, :], axis=-1)


def local_pair(mats, vecs, backward):
    count, width = mats.shape[0], mats.shape[-1]
    pm = mats.reshape(count // 2, 2, width, width)
    pv = vecs.reshape(count // 2, 2, width)
    first, second = (1, 0) if backward else (0, 1)
    joined = mm(pm[:, second], pm[:, first])
    partner = jnp.stack((pv[:, 1], pv[:, 0]), axis=1).reshape(count, width)
    crossed = mv_whole(mats, partner).reshape(count // 2, 2, width)
    return joined, crossed[:, second] + pv[:, second]


def pair_up(mats, vecs, backward):
    shape = mats.shape
    pm = mats.reshape(shape[:-3] + (shape[-3] // 2, 2) + shape[-2:])
    pv = vecs.reshape(vecs.shape[:-2] + (vecs.shape[-2] // 2, 2, vecs.shape[-1]))
    first, second = (1, 0) if backward else (0, 1)
    m1, m2 = pm[..., first, :, :], pm[..., second, :, :]
    v1, v2 = pv[..., first, :], pv[..., second, :]
    return mm(m2, m1), mv(m2, v1) + v2


def local_tiers(mats, vecs, backward, joined=None):
    tiers = [(mats, vecs)]
    if joined is not None:
        count, width = mats.shape[0], mats.shape[-1]
        pv = vecs.reshape(count // 2, 2, width)
        partner = jnp.stack((pv[:, 1], pv[:, 0]), axis=1).reshape(count, width)
        crossed = mv_whole(mats, partner).reshape(count // 2, 2, width)
        second = 0 if backward else 1
        tiers.append((joined, crossed[:, second] + pv[:, second]))
    while tiers[-1][0].shape[0] > 1:
        tiers.append(local_pair(tiers[-1][0], tiers[-1][1], backward))
    return tiers


def spread(tiers, entry, backward):
    width = entry.shape[0]
    states = entry[None, :]
    for height in reversed(range(len(tiers) - 1)):
        mats, vecs = tiers[height]
        half = mats.shape[0] // 2
        pv = vecs.reshape(half, 2, width)
        both = jnp.broadcast_to(states[:, None, :], (half, 2, width)).reshape(-1, width)
        applied = mv_whole(mats, both).reshape(half, 2, width)
        if backward:
            other = applied[:, 1] + pv[:, 1]
            states = jnp.stack((other, states), axis=1)
        else:
            other = applied[:, 0] + pv[:, 0]
            states = jnp.stack((states, other), axis=1)
        states = states.reshape(-1, width)
    return mv_whole(tiers[0][0], states) + tiers[0][1]


def pad_pow2(mats, vecs):
    count = mats.shape[-3]
    size = 1
    while size < count:
        size *= 2
    if size > count:
        width = mats.shape[-1]
        eye = jnp.broadcast_to(
            jnp.eye(width, dtype=mats.dtype), mats.shape[:-3] + (size - count, width, width)
        )
        mats = jnp.concatenate((mats, eye), axis=-3)
        zero = jnp.zeros(vecs.shape[:-2] + (size - count, width), vecs.dtype)
        vecs = jnp.concatenate((vecs, zero), axis=-2)
    return mats, vecs


def reduce_maps(mats, vecs, backward):
    mats, vecs = pad_pow2(mats, vecs)
    while mats.shape[-3] > 1:
        mats, vecs = local_pair(mats, vecs, backward)
    return mats[..., 0, :, :], vecs[..., 0, :]


def keep_only(mats, vecs, keep):
    eye = jnp.eye(mats.shape[-1], dtype=jnp.float32)
    mats = jnp.where(keep[:, None, None], mats, eye)
    vecs = jnp.where(keep[:, None], vecs, 0.0)
    return mats, vecs


def pack(mat, vec):
    return jnp.concatenate((mat, vec[None, :]), axis=0)


def from_other_groups(packed, backward):
    count = lax.axis_size("outer")
    me = lax.axis_index("outer")
    received = []
    keep = []
    for shift in reversed(range(1, count)):
        step = -shift if backward else shift
        pairs = [(i, (i + step) % count) for i in range(count)]
        received.append(lax.ppermute(packed, "outer", pairs))
        keep.append(me + shift <= count - 1 if backward else me - shift >= 0)
    return received, keep


def across(mat, vec, start, backward):
    gathered = lax.all_gather(pack(mat, vec), "inner")
    mats, vecs = gathered[:, :-1], gathered[:, -1]
    gm, gv = reduce_maps(mats, vecs, backward)
    received, keep = from_other_groups(pack(gm, gv), backward)
    me = lax.axis_index("inner")
    index = jnp.arange(mats.shape[0])
    mine = index > me if backward else index < me
    pm, pv = reduce_maps(*keep_only(mats, vecs, mine), backward)
    eye = jnp.eye(mat.shape[-1], dtype=jnp.float32)
    state = start
    for block, kept in zip(received, keep):
        state = mv_whole(jnp.where(kept, block[:-1], eye), state) + jnp.where(kept, block[-1], 0.0)
    return mv_whole(pm, state) + pv


def on_device(observations, gains, smoother_gains, transition, observation_map, initial_mean):
    me = lax.axis_index(AXES)
    devices = lax.axis_size(AXES)
    width = smoother_gains.shape[-1]
    paired = smoother_gains.reshape(smoother_gains.shape[0] // 2, 2, width, width)
    back_joined = lax.optimization_barrier(mm(paired[:, 0], paired[:, 1]))
    mapped = mm(observation_map, transition)
    forward_maps = transition[None] - jnp.einsum(
        "tij,jk->tik", gains, mapped, precision=exact, preferred_element_type=jnp.float32
    )
    forward_inputs = mv_whole(gains, observations)
    forward = local_tiers(forward_maps, forward_inputs, False)
    fm, fv = forward[-1][0][0], forward[-1][1][0]
    entry_state = across(fm, fv, initial_mean, False)
    filtered = spread(forward, entry_state, False)

    predicted_all = jnp.dot(
        filtered, transition.T, precision=exact, preferred_element_type=jnp.float32
    )
    offsets = filtered - mv_whole(smoother_gains, predicted_all)
    backward = local_tiers(smoother_gains, offsets, True, back_joined)
    bm, bv = backward[-1][0][0], backward[-1][1][0]
    last = me == devices - 1
    extra = jnp.where(last, predicted_all[-1], 0.0)
    bv = bv + mv_whole(bm, extra)
    after_state = across(bm, bv, jnp.zeros_like(extra), True) + extra
    smoothed = spread(backward, after_state, True)
    return (filtered, smoothed)


def solution(mesh):
    in_specs = (
        P(AXES, None),
        P(AXES, None, None),
        P(AXES, None, None),
        P(),
        P(),
        P(),
    )
    out_specs = (P(AXES, None), P(AXES, None))
    return jax.shard_map(
        on_device, mesh=mesh, in_specs=in_specs, out_specs=out_specs, check_vma=False
    )
```

```python
import jax
import jax.numpy as jnp
from jax import lax
from jax.sharding import PartitionSpec as P

exact = lax.Precision.HIGHEST
AXES = ("outer", "inner")


def mm(a, b):
    return jnp.matmul(a, b, precision=exact, preferred_element_type=jnp.float32)


def mv(a, v):
    return jnp.einsum("...ij,...j->...i", a, v, precision=exact, preferred_element_type=jnp.float32)


def mv_whole(a, v):
    return jnp.sum(a * v[..., None, :], axis=-1)


def local_pair(mats, vecs, backward):
    count, width = mats.shape[0], mats.shape[-1]
    pm = mats.reshape(count // 2, 2, width, width)
    pv = vecs.reshape(count // 2, 2, width)
    first, second = (1, 0) if backward else (0, 1)
    joined = mm(pm[:, second], pm[:, first])
    partner = jnp.stack((pv[:, 1], pv[:, 0]), axis=1).reshape(count, width)
    crossed = mv_whole(mats, partner).reshape(count // 2, 2, width)
    return joined, crossed[:, second] + pv[:, second]


def pair_up(mats, vecs, backward):
    shape = mats.shape
    pm = mats.reshape(shape[:-3] + (shape[-3] // 2, 2) + shape[-2:])
    pv = vecs.reshape(vecs.shape[:-2] + (vecs.shape[-2] // 2, 2, vecs.shape[-1]))
    first, second = (1, 0) if backward else (0, 1)
    m1, m2 = pm[..., first, :, :], pm[..., second, :, :]
    v1, v2 = pv[..., first, :], pv[..., second, :]
    return mm(m2, m1), mv(m2, v1) + v2


def local_tiers(mats, vecs, backward):
    tiers = [(mats, vecs)]
    while tiers[-1][0].shape[0] > 1:
        tiers.append(local_pair(tiers[-1][0], tiers[-1][1], backward))
    return tiers


def spread(tiers, entry, backward):
    width = entry.shape[0]
    states = entry[None, :]
    for height in reversed(range(len(tiers) - 1)):
        mats, vecs = tiers[height]
        half = mats.shape[0] // 2
        pv = vecs.reshape(half, 2, width)
        rows = mats.reshape(half, 2 * width, width)
        if backward:
            other = mv_whole(rows[:, width:], states) + pv[:, 1]
            states = jnp.stack((other, states), axis=1)
        else:
            other = mv_whole(rows[:, :width], states) + pv[:, 0]
            states = jnp.stack((states, other), axis=1)
        states = states.reshape(-1, width)
    return mv_whole(tiers[0][0], states) + tiers[0][1]


def pad_pow2(mats, vecs):
    count = mats.shape[-3]
    size = 1
    while size < count:
        size *= 2
    if size > count:
        width = mats.shape[-1]
        eye = jnp.broadcast_to(
            jnp.eye(width, dtype=mats.dtype), mats.shape[:-3] + (size - count, width, width)
        )
        mats = jnp.concatenate((mats, eye), axis=-3)
        zero = jnp.zeros(vecs.shape[:-2] + (size - count, width), vecs.dtype)
        vecs = jnp.concatenate((vecs, zero), axis=-2)
    return mats, vecs


def reduce_maps(mats, vecs, backward):
    mats, vecs = pad_pow2(mats, vecs)
    while mats.shape[-3] > 1:
        mats, vecs = local_pair(mats, vecs, backward)
    return mats[..., 0, :, :], vecs[..., 0, :]


def keep_only(mats, vecs, keep):
    eye = jnp.eye(mats.shape[-1], dtype=jnp.float32)
    mats = jnp.where(keep[:, None, None], mats, eye)
    vecs = jnp.where(keep[:, None], vecs, 0.0)
    return mats, vecs


def pack(mat, vec):
    return jnp.concatenate((mat, vec[None, :]), axis=0)


def from_other_groups(packed, backward):
    count = lax.axis_size("outer")
    me = lax.axis_index("outer")
    received = []
    keep = []
    for shift in reversed(range(1, count)):
        step = -shift if backward else shift
        pairs = [(i, (i + step) % count) for i in range(count)]
        received.append(lax.ppermute(packed, "outer", pairs))
        keep.append(me + shift <= count - 1 if backward else me - shift >= 0)
    return received, keep


def across(mat, vec, start, backward):
    gathered = lax.all_gather(pack(mat, vec), "inner")
    mats, vecs = gathered[:, :-1], gathered[:, -1]
    gm, gv = reduce_maps(mats, vecs, backward)
    received, keep = from_other_groups(pack(gm, gv), backward)
    me = lax.axis_index("inner")
    index = jnp.arange(mats.shape[0])
    mine = index > me if backward else index < me
    pm, pv = reduce_maps(*keep_only(mats, vecs, mine), backward)
    eye = jnp.eye(mat.shape[-1], dtype=jnp.float32)
    state = start
    for block, kept in zip(received, keep):
        state = mv_whole(jnp.where(kept, block[:-1], eye), state) + jnp.where(kept, block[-1], 0.0)
    return mv_whole(pm, state) + pv


def on_device(observations, gains, smoother_gains, transition, observation_map, initial_mean):
    me = lax.axis_index(AXES)
    devices = lax.axis_size(AXES)
    mapped = mm(observation_map, transition)
    forward_maps = transition[None] - jnp.einsum(
        "tij,jk->tik", gains, mapped, precision=exact, preferred_element_type=jnp.float32
    )
    forward_inputs = mv_whole(gains, observations)
    forward = local_tiers(forward_maps, forward_inputs, False)
    fm, fv = forward[-1][0][0], forward[-1][1][0]
    entry_state = across(fm, fv, initial_mean, False)
    filtered = spread(forward, entry_state, False)

    predicted_all = jnp.dot(
        filtered, transition.T, precision=exact, preferred_element_type=jnp.float32
    )
    offsets = filtered - mv_whole(smoother_gains, predicted_all)
    backward = local_tiers(smoother_gains, offsets, True)
    bm, bv = backward[-1][0][0], backward[-1][1][0]
    last = me == devices - 1
    extra = jnp.where(last, predicted_all[-1], 0.0)
    bv = bv + mv_whole(bm, extra)
    after_state = across(bm, bv, jnp.zeros_like(extra), True) + extra
    smoothed = spread(backward, after_state, True)
    return (filtered, smoothed)


def solution(mesh):
    in_specs = (
        P(AXES, None),
        P(AXES, None, None),
        P(AXES, None, None),
        P(),
        P(),
        P(),
    )
    out_specs = (P(AXES, None), P(AXES, None))
    return jax.shard_map(
        on_device, mesh=mesh, in_specs=in_specs, out_specs=out_specs, check_vma=False
    )
```

```python
import jax
import jax.numpy as jnp
from jax import lax
from jax.sharding import PartitionSpec as P

exact = lax.Precision.HIGHEST
AXES = ("outer", "inner")


def mm(a, b):
    return jnp.matmul(a, b, precision=exact, preferred_element_type=jnp.float32)


def mv(a, v):
    return jnp.einsum("...ij,...j->...i", a, v, precision=exact, preferred_element_type=jnp.float32)


def mv_whole(a, v):
    return jnp.sum(a * v[..., None, :], axis=-1)


def local_pair(mats, vecs, backward):
    count, width = mats.shape[0], mats.shape[-1]
    pm = mats.reshape(count // 2, 2, width, width)
    pv = vecs.reshape(count // 2, 2, width)
    first, second = (1, 0) if backward else (0, 1)
    joined = mm(pm[:, second], pm[:, first])
    rows = mats.reshape(count // 2, 2 * width, width)
    later = rows[:, width:] if second == 1 else rows[:, :width]
    return joined, mv_whole(later, pv[:, first]) + pv[:, second]


def pair_up(mats, vecs, backward):
    shape = mats.shape
    pm = mats.reshape(shape[:-3] + (shape[-3] // 2, 2) + shape[-2:])
    pv = vecs.reshape(vecs.shape[:-2] + (vecs.shape[-2] // 2, 2, vecs.shape[-1]))
    first, second = (1, 0) if backward else (0, 1)
    m1, m2 = pm[..., first, :, :], pm[..., second, :, :]
    v1, v2 = pv[..., first, :], pv[..., second, :]
    return mm(m2, m1), mv(m2, v1) + v2


def local_tiers(mats, vecs, backward):
    tiers = [(mats, vecs)]
    while tiers[-1][0].shape[0] > 1:
        tiers.append(local_pair(tiers[-1][0], tiers[-1][1], backward))
    return tiers


def spread(tiers, entry, backward):
    width = entry.shape[0]
    states = entry[None, :]
    for height in reversed(range(len(tiers) - 1)):
        mats, vecs = tiers[height]
        half = mats.shape[0] // 2
        pv = vecs.reshape(half, 2, width)
        rows = mats.reshape(half, 2 * width, width)
        if backward:
            other = mv_whole(rows[:, width:], states) + pv[:, 1]
            states = jnp.stack((other, states), axis=1)
        else:
            other = mv_whole(rows[:, :width], states) + pv[:, 0]
            states = jnp.stack((states, other), axis=1)
        states = states.reshape(-1, width)
    return mv_whole(tiers[0][0], states) + tiers[0][1]


def pad_pow2(mats, vecs):
    count = mats.shape[-3]
    size = 1
    while size < count:
        size *= 2
    if size > count:
        width = mats.shape[-1]
        eye = jnp.broadcast_to(
            jnp.eye(width, dtype=mats.dtype), mats.shape[:-3] + (size - count, width, width)
        )
        mats = jnp.concatenate((mats, eye), axis=-3)
        zero = jnp.zeros(vecs.shape[:-2] + (size - count, width), vecs.dtype)
        vecs = jnp.concatenate((vecs, zero), axis=-2)
    return mats, vecs


def reduce_maps(mats, vecs, backward):
    mats, vecs = pad_pow2(mats, vecs)
    while mats.shape[-3] > 1:
        mats, vecs = local_pair(mats, vecs, backward)
    return mats[..., 0, :, :], vecs[..., 0, :]


def keep_only(mats, vecs, keep):
    eye = jnp.eye(mats.shape[-1], dtype=jnp.float32)
    mats = jnp.where(keep[:, None, None], mats, eye)
    vecs = jnp.where(keep[:, None], vecs, 0.0)
    return mats, vecs


def pack(mat, vec):
    return jnp.concatenate((mat, vec[None, :]), axis=0)


def from_other_groups(packed, backward):
    count = lax.axis_size("outer")
    me = lax.axis_index("outer")
    received = []
    keep = []
    for shift in reversed(range(1, count)):
        step = -shift if backward else shift
        pairs = [(i, (i + step) % count) for i in range(count)]
        received.append(lax.ppermute(packed, "outer", pairs))
        keep.append(me + shift <= count - 1 if backward else me - shift >= 0)
    return received, keep


def across(mat, vec, start, backward):
    gathered = lax.all_gather(pack(mat, vec), "inner")
    mats, vecs = gathered[:, :-1], gathered[:, -1]
    gm, gv = reduce_maps(mats, vecs, backward)
    received, keep = from_other_groups(pack(gm, gv), backward)
    me = lax.axis_index("inner")
    index = jnp.arange(mats.shape[0])
    mine = index > me if backward else index < me
    pm, pv = reduce_maps(*keep_only(mats, vecs, mine), backward)
    eye = jnp.eye(mat.shape[-1], dtype=jnp.float32)
    state = start
    for block, kept in zip(received, keep):
        state = mv_whole(jnp.where(kept, block[:-1], eye), state) + jnp.where(kept, block[-1], 0.0)
    return mv_whole(pm, state) + pv


def on_device(observations, gains, smoother_gains, transition, observation_map, initial_mean):
    me = lax.axis_index(AXES)
    devices = lax.axis_size(AXES)
    mapped = mm(observation_map, transition)
    forward_maps = transition[None] - jnp.einsum(
        "tij,jk->tik", gains, mapped, precision=exact, preferred_element_type=jnp.float32
    )
    forward_inputs = mv_whole(gains, observations)
    forward = local_tiers(forward_maps, forward_inputs, False)
    fm, fv = forward[-1][0][0], forward[-1][1][0]
    entry_state = across(fm, fv, initial_mean, False)
    filtered = spread(forward, entry_state, False)

    predicted_all = jnp.dot(
        filtered, transition.T, precision=exact, preferred_element_type=jnp.float32
    )
    offsets = filtered - mv_whole(smoother_gains, predicted_all)
    backward = local_tiers(smoother_gains, offsets, True)
    bm, bv = backward[-1][0][0], backward[-1][1][0]
    last = me == devices - 1
    extra = jnp.where(last, predicted_all[-1], 0.0)
    bv = bv + mv_whole(bm, extra)
    after_state = across(bm, bv, jnp.zeros_like(extra), True) + extra
    smoothed = spread(backward, after_state, True)
    return (filtered, smoothed)


def solution(mesh):
    in_specs = (
        P(AXES, None),
        P(AXES, None, None),
        P(AXES, None, None),
        P(),
        P(),
        P(),
    )
    out_specs = (P(AXES, None), P(AXES, None))
    return jax.shard_map(
        on_device, mesh=mesh, in_specs=in_specs, out_specs=out_specs, check_vma=False
    )
```

```python
import jax
import jax.numpy as jnp
from jax import lax
from jax.sharding import PartitionSpec as P

exact = lax.Precision.HIGHEST
AXES = ("outer", "inner")


def mm(a, b):
    return jnp.matmul(a, b, precision=exact, preferred_element_type=jnp.float32)


def mv(a, v):
    return jnp.einsum("...ij,...j->...i", a, v, precision=exact, preferred_element_type=jnp.float32)


def mv_whole(a, v):
    return jnp.sum(a * v[..., None, :], axis=-1)


def local_pair(mats, vecs, backward, whole=True):
    count, width = mats.shape[0], mats.shape[-1]
    pm = mats.reshape(count // 2, 2, width, width)
    pv = vecs.reshape(count // 2, 2, width)
    first, second = (1, 0) if backward else (0, 1)
    joined = mm(pm[:, second], pm[:, first])
    if not whole:
        rows = mats.reshape(count // 2, 2 * width, width)
        later = rows[:, width:] if second == 1 else rows[:, :width]
        return joined, mv_whole(later, pv[:, first]) + pv[:, second]
    partner = jnp.stack((pv[:, 1], pv[:, 0]), axis=1).reshape(count, width)
    crossed = mv_whole(mats, partner).reshape(count // 2, 2, width)
    return joined, crossed[:, second] + pv[:, second]


def pair_up(mats, vecs, backward):
    shape = mats.shape
    pm = mats.reshape(shape[:-3] + (shape[-3] // 2, 2) + shape[-2:])
    pv = vecs.reshape(vecs.shape[:-2] + (vecs.shape[-2] // 2, 2, vecs.shape[-1]))
    first, second = (1, 0) if backward else (0, 1)
    m1, m2 = pm[..., first, :, :], pm[..., second, :, :]
    v1, v2 = pv[..., first, :], pv[..., second, :]
    return mm(m2, m1), mv(m2, v1) + v2


def local_tiers(mats, vecs, backward):
    tiers = [(mats, vecs)]
    while tiers[-1][0].shape[0] > 1:
        tiers.append(local_pair(tiers[-1][0], tiers[-1][1], backward))
    return tiers


def spread(tiers, entry, backward):
    width = entry.shape[0]
    states = entry[None, :]
    for height in reversed(range(len(tiers) - 1)):
        mats, vecs = tiers[height]
        half = mats.shape[0] // 2
        pv = vecs.reshape(half, 2, width)
        rows = mats.reshape(half, 2 * width, width)
        if backward:
            other = mv_whole(rows[:, width:], states) + pv[:, 1]
            states = jnp.stack((other, states), axis=1)
        else:
            other = mv_whole(rows[:, :width], states) + pv[:, 0]
            states = jnp.stack((states, other), axis=1)
        states = states.reshape(-1, width)
    return mv_whole(tiers[0][0], states) + tiers[0][1]


def pad_pow2(mats, vecs):
    count = mats.shape[-3]
    size = 1
    while size < count:
        size *= 2
    if size > count:
        width = mats.shape[-1]
        eye = jnp.broadcast_to(
            jnp.eye(width, dtype=mats.dtype), mats.shape[:-3] + (size - count, width, width)
        )
        mats = jnp.concatenate((mats, eye), axis=-3)
        zero = jnp.zeros(vecs.shape[:-2] + (size - count, width), vecs.dtype)
        vecs = jnp.concatenate((vecs, zero), axis=-2)
    return mats, vecs


def reduce_maps(mats, vecs, backward):
    mats, vecs = pad_pow2(mats, vecs)
    while mats.shape[-3] > 1:
        mats, vecs = local_pair(mats, vecs, backward, whole=False)
    return mats[..., 0, :, :], vecs[..., 0, :]


def keep_only(mats, vecs, keep):
    eye = jnp.eye(mats.shape[-1], dtype=jnp.float32)
    mats = jnp.where(keep[:, None, None], mats, eye)
    vecs = jnp.where(keep[:, None], vecs, 0.0)
    return mats, vecs


def pack(mat, vec):
    return jnp.concatenate((mat, vec[None, :]), axis=0)


def from_other_groups(packed, backward):
    count = lax.axis_size("outer")
    me = lax.axis_index("outer")
    received = []
    keep = []
    for shift in reversed(range(1, count)):
        step = -shift if backward else shift
        pairs = [(i, (i + step) % count) for i in range(count)]
        received.append(lax.ppermute(packed, "outer", pairs))
        keep.append(me + shift <= count - 1 if backward else me - shift >= 0)
    return received, keep


def across(mat, vec, start, backward):
    gathered = lax.all_gather(pack(mat, vec), "inner")
    mats, vecs = gathered[:, :-1], gathered[:, -1]
    gm, gv = reduce_maps(mats, vecs, backward)
    received, keep = from_other_groups(pack(gm, gv), backward)
    me = lax.axis_index("inner")
    index = jnp.arange(mats.shape[0])
    mine = index > me if backward else index < me
    pm, pv = reduce_maps(*keep_only(mats, vecs, mine), backward)
    eye = jnp.eye(mat.shape[-1], dtype=jnp.float32)
    state = start
    for block, kept in zip(received, keep):
        state = mv_whole(jnp.where(kept, block[:-1], eye), state) + jnp.where(kept, block[-1], 0.0)
    return mv_whole(pm, state) + pv


def on_device(observations, gains, smoother_gains, transition, observation_map, initial_mean):
    me = lax.axis_index(AXES)
    devices = lax.axis_size(AXES)
    mapped = mm(observation_map, transition)
    forward_maps = transition[None] - jnp.einsum(
        "tij,jk->tik", gains, mapped, precision=exact, preferred_element_type=jnp.float32
    )
    forward_inputs = mv_whole(gains, observations)
    forward = local_tiers(forward_maps, forward_inputs, False)
    fm, fv = forward[-1][0][0], forward[-1][1][0]
    entry_state = across(fm, fv, initial_mean, False)
    filtered = spread(forward, entry_state, False)

    predicted_all = jnp.dot(
        filtered, transition.T, precision=exact, preferred_element_type=jnp.float32
    )
    offsets = filtered - mv_whole(smoother_gains, predicted_all)
    backward = local_tiers(smoother_gains, offsets, True)
    bm, bv = backward[-1][0][0], backward[-1][1][0]
    last = me == devices - 1
    extra = jnp.where(last, predicted_all[-1], 0.0)
    bv = bv + mv_whole(bm, extra)
    after_state = across(bm, bv, jnp.zeros_like(extra), True) + extra
    smoothed = spread(backward, after_state, True)
    return (filtered, smoothed)


def solution(mesh):
    in_specs = (
        P(AXES, None),
        P(AXES, None, None),
        P(AXES, None, None),
        P(),
        P(),
        P(),
    )
    out_specs = (P(AXES, None), P(AXES, None))
    return jax.shard_map(
        on_device, mesh=mesh, in_specs=in_specs, out_specs=out_specs, check_vma=False
    )
```

```python
import jax
import jax.numpy as jnp
from jax import lax
from jax.sharding import PartitionSpec as P

exact = lax.Precision.HIGHEST
AXES = ("outer", "inner")


def mm(a, b):
    return jnp.matmul(a, b, precision=exact, preferred_element_type=jnp.float32)


def mv(a, v):
    return jnp.einsum("...ij,...j->...i", a, v, precision=exact, preferred_element_type=jnp.float32)


def mv_whole(a, v):
    return jnp.sum(a * v[..., None, :], axis=-1)


def local_pair(mats, vecs, backward):
    count, width = mats.shape[0], mats.shape[-1]
    pm = mats.reshape(count // 2, 2, width, width)
    pv = vecs.reshape(count // 2, 2, width)
    first, second = (1, 0) if backward else (0, 1)
    joined = mm(pm[:, second], pm[:, first])
    partner = jnp.stack((pv[:, 1], pv[:, 0]), axis=1).reshape(count, width)
    crossed = mv_whole(mats, partner).reshape(count // 2, 2, width)
    return joined, crossed[:, second] + pv[:, second]


def pair_up(mats, vecs, backward):
    shape = mats.shape
    pm = mats.reshape(shape[:-3] + (shape[-3] // 2, 2) + shape[-2:])
    pv = vecs.reshape(vecs.shape[:-2] + (vecs.shape[-2] // 2, 2, vecs.shape[-1]))
    first, second = (1, 0) if backward else (0, 1)
    m1, m2 = pm[..., first, :, :], pm[..., second, :, :]
    v1, v2 = pv[..., first, :], pv[..., second, :]
    return mm(m2, m1), mv(m2, v1) + v2


def local_tiers(mats, vecs, backward):
    tiers = [(mats, vecs)]
    while tiers[-1][0].shape[0] > 1:
        tiers.append(local_pair(tiers[-1][0], tiers[-1][1], backward))
    return tiers


def spread(tiers, entry, backward):
    width = entry.shape[0]
    states = entry[None, :]
    for height in reversed(range(len(tiers) - 1)):
        mats, vecs = tiers[height]
        half = mats.shape[0] // 2
        pv = vecs.reshape(half, 2, width)
        rows = mats.reshape(half, 2 * width, width)
        if backward:
            other = mv_whole(rows[:, width:], states) + pv[:, 1]
            states = jnp.stack((other, states), axis=1)
        else:
            other = mv_whole(rows[:, :width], states) + pv[:, 0]
            states = jnp.stack((states, other), axis=1)
        states = states.reshape(-1, width)
    return mv_whole(tiers[0][0], states) + tiers[0][1]


def pad_pow2(mats, vecs):
    count = mats.shape[-3]
    size = 1
    while size < count:
        size *= 2
    if size > count:
        width = mats.shape[-1]
        eye = jnp.broadcast_to(
            jnp.eye(width, dtype=mats.dtype), mats.shape[:-3] + (size - count, width, width)
        )
        mats = jnp.concatenate((mats, eye), axis=-3)
        zero = jnp.zeros(vecs.shape[:-2] + (size - count, width), vecs.dtype)
        vecs = jnp.concatenate((vecs, zero), axis=-2)
    return mats, vecs


def reduce_maps(mats, vecs, backward):
    mats, vecs = pad_pow2(mats, vecs)
    while mats.shape[-3] > 1:
        mats, vecs = local_pair(mats, vecs, backward)
    return mats[..., 0, :, :], vecs[..., 0, :]


def keep_only(mats, vecs, keep):
    eye = jnp.eye(mats.shape[-1], dtype=jnp.float32)
    mats = jnp.where(keep[:, None, None], mats, eye)
    vecs = jnp.where(keep[:, None], vecs, 0.0)
    return mats, vecs


def pack(mat, vec):
    return jnp.concatenate((mat, vec[None, :]), axis=0)


def from_other_groups(packed, backward):
    count = lax.axis_size("outer")
    me = lax.axis_index("outer")
    received = []
    keep = []
    for shift in reversed(range(1, count)):
        step = -shift if backward else shift
        pairs = [(i, (i + step) % count) for i in range(count)]
        received.append(lax.ppermute(packed, "outer", pairs))
        keep.append(me + shift <= count - 1 if backward else me - shift >= 0)
    return received, keep


def across(mat, vec, start, backward):
    gathered = lax.all_gather(pack(mat, vec), "inner")
    mats, vecs = gathered[:, :-1], gathered[:, -1]
    gm, gv = reduce_maps(mats, vecs, backward)
    received, keep = from_other_groups(pack(gm, gv), backward)
    me = lax.axis_index("inner")
    index = jnp.arange(mats.shape[0])
    mine = index > me if backward else index < me
    pm, pv = reduce_maps(*keep_only(mats, vecs, mine), backward)
    eye = jnp.eye(mat.shape[-1], dtype=jnp.float32)
    state = start
    for block, kept in zip(received, keep):
        state = mv_whole(jnp.where(kept, block[:-1], eye), state) + jnp.where(kept, block[-1], 0.0)
    return mv_whole(pm, state) + pv


def on_device(observations, gains, smoother_gains, transition, observation_map, initial_mean):
    me = lax.axis_index(AXES)
    devices = lax.axis_size(AXES)
    mapped = mm(observation_map, transition)
    forward_maps = transition[None] - jnp.einsum(
        "tij,jk->tik", gains, mapped, precision=exact, preferred_element_type=jnp.float32
    )
    forward_inputs = mv_whole(gains, observations)
    forward = local_tiers(forward_maps, forward_inputs, False)
    fm, fv = forward[-1][0][0], forward[-1][1][0]
    entry_state = across(fm, fv, initial_mean, False)
    filtered = spread(forward, entry_state, False)

    predicted_all = mv_whole(transition[None], filtered)
    offsets = filtered - mv_whole(smoother_gains, predicted_all)
    backward = local_tiers(smoother_gains, offsets, True)
    bm, bv = backward[-1][0][0], backward[-1][1][0]
    last = me == devices - 1
    extra = jnp.where(last, predicted_all[-1], 0.0)
    bv = bv + mv_whole(bm, extra)
    after_state = across(bm, bv, jnp.zeros_like(extra), True) + extra
    smoothed = spread(backward, after_state, True)
    return (filtered, smoothed)


def solution(mesh):
    in_specs = (
        P(AXES, None),
        P(AXES, None, None),
        P(AXES, None, None),
        P(),
        P(),
        P(),
    )
    out_specs = (P(AXES, None), P(AXES, None))
    return jax.shard_map(
        on_device, mesh=mesh, in_specs=in_specs, out_specs=out_specs, check_vma=False
    )
```

```python
import jax
import jax.numpy as jnp
from jax import lax
from jax.sharding import PartitionSpec as P

exact = lax.Precision.HIGHEST
AXES = ("outer", "inner")


def mm(a, b):
    return jnp.matmul(a, b, precision=exact, preferred_element_type=jnp.float32)


def mv(a, v):
    return jnp.einsum("...ij,...j->...i", a, v, precision=exact, preferred_element_type=jnp.float32)


def mv_whole(a, v):
    return jnp.sum(a * v[..., None, :], axis=-1)


def local_pair(mats, vecs, backward):
    count, width = mats.shape[0], mats.shape[-1]
    pm = mats.reshape(count // 2, 2, width, width)
    pv = vecs.reshape(count // 2, 2, width)
    first, second = (1, 0) if backward else (0, 1)
    joined = mm(pm[:, second], pm[:, first])
    partner = jnp.stack((pv[:, 1], pv[:, 0]), axis=1).reshape(count, width)
    crossed = mv_whole(mats, partner).reshape(count // 2, 2, width)
    return joined, crossed[:, second] + pv[:, second]


def pair_up(mats, vecs, backward):
    shape = mats.shape
    pm = mats.reshape(shape[:-3] + (shape[-3] // 2, 2) + shape[-2:])
    pv = vecs.reshape(vecs.shape[:-2] + (vecs.shape[-2] // 2, 2, vecs.shape[-1]))
    first, second = (1, 0) if backward else (0, 1)
    m1, m2 = pm[..., first, :, :], pm[..., second, :, :]
    v1, v2 = pv[..., first, :], pv[..., second, :]
    return mm(m2, m1), mv(m2, v1) + v2


def local_tiers(mats, vecs, backward):
    tiers = [(mats, vecs)]
    while tiers[-1][0].shape[0] > 1:
        tiers.append(local_pair(tiers[-1][0], tiers[-1][1], backward))
    return tiers


def spread(tiers, entry, backward):
    width = entry.shape[0]
    states = entry[None, :]
    for height in reversed(range(len(tiers) - 1)):
        mats, vecs = tiers[height]
        half = mats.shape[0] // 2
        pv = vecs.reshape(half, 2, width)
        rows = mats.reshape(half, 2 * width, width)
        if backward:
            other = mv_whole(rows[:, width:], states) + pv[:, 1]
            states = jnp.stack((other, states), axis=1)
        else:
            other = mv_whole(rows[:, :width], states) + pv[:, 0]
            states = jnp.stack((states, other), axis=1)
        states = states.reshape(-1, width)
    return mv_whole(tiers[0][0], states) + tiers[0][1]


def pad_pow2(mats, vecs):
    count = mats.shape[-3]
    size = 1
    while size < count:
        size *= 2
    if size > count:
        width = mats.shape[-1]
        eye = jnp.broadcast_to(
            jnp.eye(width, dtype=mats.dtype), mats.shape[:-3] + (size - count, width, width)
        )
        mats = jnp.concatenate((mats, eye), axis=-3)
        zero = jnp.zeros(vecs.shape[:-2] + (size - count, width), vecs.dtype)
        vecs = jnp.concatenate((vecs, zero), axis=-2)
    return mats, vecs


def reduce_maps(mats, vecs, backward):
    mats, vecs = pad_pow2(mats, vecs)
    while mats.shape[-3] > 1:
        mats, vecs = local_pair(mats, vecs, backward)
    return mats[..., 0, :, :], vecs[..., 0, :]


def keep_only(mats, vecs, keep):
    eye = jnp.eye(mats.shape[-1], dtype=jnp.float32)
    mats = jnp.where(keep[:, None, None], mats, eye)
    vecs = jnp.where(keep[:, None], vecs, 0.0)
    return mats, vecs


def pack(mat, vec):
    return jnp.concatenate((mat, vec[None, :]), axis=0)


def from_other_groups(packed, backward):
    count = lax.axis_size("outer")
    me = lax.axis_index("outer")
    received = []
    keep = []
    for shift in reversed(range(1, count)):
        step = -shift if backward else shift
        pairs = [(i, (i + step) % count) for i in range(count)]
        received.append(lax.ppermute(packed, "outer", pairs))
        keep.append(me + shift <= count - 1 if backward else me - shift >= 0)
    return received, keep


def across(mat, vec, start, backward):
    gathered = lax.all_gather(pack(mat, vec), "inner")
    mats, vecs = gathered[:, :-1], gathered[:, -1]
    gm, gv = reduce_maps(mats, vecs, backward)
    received, keep = from_other_groups(pack(gm, gv), backward)
    me = lax.axis_index("inner")
    index = jnp.arange(mats.shape[0])
    mine = index > me if backward else index < me
    pm, pv = reduce_maps(*keep_only(mats, vecs, mine), backward)
    eye = jnp.eye(mat.shape[-1], dtype=jnp.float32)
    state = start
    for block, kept in zip(received, keep):
        state = mv_whole(jnp.where(kept, block[:-1], eye), state) + jnp.where(kept, block[-1], 0.0)
    return mv_whole(pm, state) + pv


def on_device(observations, gains, smoother_gains, transition, observation_map, initial_mean):
    me = lax.axis_index(AXES)
    devices = lax.axis_size(AXES)
    mapped = mm(observation_map, transition)
    forward_maps = transition[None] - jnp.einsum(
        "tij,jk->tik", gains, mapped, precision=exact, preferred_element_type=jnp.float32
    )
    forward_inputs = mv_whole(gains, observations)
    forward = local_tiers(forward_maps, forward_inputs, False)
    fm, fv = forward[-1][0][0], forward[-1][1][0]
    entry_state = across(fm, fv, initial_mean, False)
    filtered = spread(forward, entry_state, False)

    predicted_all = jnp.dot(
        filtered, transition.T, precision=exact, preferred_element_type=jnp.float32
    )
    offsets = filtered - mv_whole(smoother_gains, predicted_all)
    final = (me == devices - 1) & (jnp.arange(offsets.shape[0]) == offsets.shape[0] - 1)
    offsets = jnp.where(final[:, None], filtered, offsets)
    backward = local_tiers(smoother_gains, offsets, True)
    bm, bv = backward[-1][0][0], backward[-1][1][0]
    after_state = across(bm, bv, jnp.zeros_like(bv), True)
    smoothed = spread(backward, after_state, True)
    return (filtered, smoothed)


def solution(mesh):
    in_specs = (
        P(AXES, None),
        P(AXES, None, None),
        P(AXES, None, None),
        P(),
        P(),
        P(),
    )
    out_specs = (P(AXES, None), P(AXES, None))
    return jax.shard_map(
        on_device, mesh=mesh, in_specs=in_specs, out_specs=out_specs, check_vma=False
    )
```
